32 devices in a mesh: seq: 16 (over z, y, core), dp: 2 (over x).
Axes of the slice: x: 2, y: 2, z: 4, core: 2. Of those that a mesh axis runs over, the one named last changes fastest.
Arguments:
- query: bfloat16 [4096, 32, 128], P(('dp', 'seq')), parts along dimension 0, may hold values from -6 to 6
- normed_key_rows: bfloat16 [4096, 16, 128], P(('dp', 'seq')), parts along dimension 0, may hold values from -6 to 6
- value_rows: bfloat16 [4096, 16, 128], P(('dp', 'seq')), parts along dimension 0, may hold values from -6 to 6
- out_in: bfloat16 [4096, 32, 128], P(('dp', 'seq')), parts along dimension 0, may hold values from -6 to 6
- grad_out: bfloat16 [4096, 32, 128], P(('dp', 'seq')), parts along dimension 0, may hold values from -6 to 6
- lse: float32 [32, 4096], P(None, ('dp', 'seq')), parts along dimension 1, may hold values from 4 to 5
Outputs:
- grad_query: bfloat16 [4096, 32, 128], P(('dp', 'seq')), parts along dimension 0
- grad_key: bfloat16 [4096, 16, 128], P(('dp', 'seq')), parts along dimension 0
- grad_value: bfloat16 [4096, 16, 128], P(('dp', 'seq')), parts along dimension 0
The draws below stay inside these ranges and needn't reach their ends.
There are 2 independent parts, one for each index of `dp`. The reference program is written for one: setup_inputs(seed, part) draws one part's arguments, and reference() takes and returns one part's arrays. A program takes and returns all parts, laid end to end along the dimension named above; each array names one. Nothing has to cross between parts.
All inputs are finite; a program needn't handle non-finite values.
Results may differ from the reference program's by a relative error of at most 0.007.
Values may be sent and summed in bfloat16 or wider, within the bound.
No kernel may reach another device: no remote copies, remote signals or barrier semaphores. Data moves between devices by JAX's collectives and lax.ppermute only.
A program may use at most 128 MiB of HBM per device.

```python
import jax
import jax.numpy as jnp
from jax import lax

HQ = 32
KEY_VALUE_HEADS = 16
HEAD_SIZE = 128
WINDOW = 1024
TOK_DEV = 128
HOPS = 8
SEQUENCE_TOKENS = 2048
N_SEQ = 16


def shard_levels(key, extent, cuts, low, largest):
    def one(dim, parts):
        heights = jax.random.uniform(jax.random.fold_in(jax.random.fold_in(key, 6), dim), (parts,), jnp.float32, low / len(cuts), largest / len(cuts))
        return jnp.repeat(jnp.exp(heights), extent[dim] // parts).reshape((-1,) + (1,) * (len(extent) - dim - 1))

    loudness = one(*cuts[0])
    for cut in cuts[1:]:
        loudness = loudness * one(*cut)
    return loudness


def gaussian(rng, shape, spread, reach, split=(), kind=jnp.bfloat16):
    result = spread * jax.random.normal(rng, shape, jnp.float32)
    if split:
        result = result * shard_levels(rng, shape, split, -0.22, 0.18)
    return jnp.clip(result, -reach, reach).astype(kind)


def setup_inputs(seed: int = 0, part: int = 0) -> dict:
    seeds = jax.random.split(jax.random.key(seed), 7)
    own_keys = jax.random.split(jax.random.fold_in(seeds[6], part), 7)
    query = gaussian(own_keys[0], (SEQUENCE_TOKENS, HQ, HEAD_SIZE), 1.0, 6.0, ((0, 16),))
    normed_key_rows = gaussian(own_keys[1], (SEQUENCE_TOKENS, KEY_VALUE_HEADS, HEAD_SIZE), 1.0, 6.0, ((0, 16),))
    value_rows = gaussian(own_keys[2], (SEQUENCE_TOKENS, KEY_VALUE_HEADS, HEAD_SIZE), 1.0, 6.0, ((0, 16),))
    out_in = gaussian(own_keys[3], (SEQUENCE_TOKENS, HQ, HEAD_SIZE), 1.0, 6.0, ((0, 16),))
    grad_out = gaussian(own_keys[4], (SEQUENCE_TOKENS, HQ, HEAD_SIZE), 1.0, 6.0, ((0, 16),))
    lse = jnp.clip(4.0 + 1.0 * jax.random.uniform(own_keys[5], (HQ, SEQUENCE_TOKENS), jnp.float32) ** shard_levels(own_keys[5], (HQ, SEQUENCE_TOKENS), ((1, 16),), -0.2, 0.2), 4.0, 5.0)
    return {"query": query, "normed_key_rows": normed_key_rows, "value_rows": value_rows, "out_in": out_in, "grad_out": grad_out, "lse": lse}


SCALE = 168.0 ** -0.5


def band_grads(q_blk, do_blk, lse_blk, delta_blk, k_win, v_win, q_start, k_start):
    tok = q_blk.shape[0]
    width = q_blk.shape[2]
    heads_kv = k_win.shape[1]
    groups = q_blk.shape[1] // heads_kv
    n_keys = k_win.shape[0]
    q_f = q_blk.reshape(tok, heads_kv, groups, width).astype(jnp.float32)
    do_f = do_blk.reshape(tok, heads_kv, groups, width).astype(jnp.float32)
    k_f = k_win.astype(jnp.float32)
    v_f = v_win.astype(jnp.float32)
    lse_r = lse_blk.reshape(heads_kv, groups, tok)
    delta_r = delta_blk.T.reshape(heads_kv, groups, tok)
    q_pos = q_start + jnp.arange(tok, dtype=jnp.int32)
    k_pos = k_start + jnp.arange(n_keys, dtype=jnp.int32)
    diff = q_pos[:, None] - k_pos[None, :]
    valid = (diff >= 0) & (diff < WINDOW) & (k_pos[None, :] >= 0)
    score = jnp.einsum('thgd,khd->hgtk', q_f, k_f) * SCALE
    prob = jnp.where(valid, jnp.exp(score - lse_r[..., None]), 0.0)
    dprob = jnp.einsum('thgd,khd->hgtk', do_f, v_f)
    dscore = prob * (dprob - delta_r[..., None])
    prob_b = lax.optimization_barrier(prob.astype(jnp.bfloat16)).astype(jnp.float32)
    dscore_b = lax.optimization_barrier(dscore.astype(jnp.bfloat16)).astype(jnp.float32)
    grad_v = jnp.einsum('hgtk,thgd->khd', prob_b, do_f)
    grad_k = jnp.einsum('hgtk,thgd->khd', dscore_b, q_f) * SCALE
    grad_q = jnp.einsum('hgtk,khd->thgd', dscore_b, k_f) * SCALE
    return grad_q.reshape(tok, heads_kv * groups, width), grad_k, grad_v


def reference(query, normed_key_rows, value_rows, out_in, grad_out, lse):
    padding_rows = HOPS * TOK_DEV
    span = (HOPS + 1) * TOK_DEV
    empty_key_value = jnp.zeros((padding_rows, KEY_VALUE_HEADS, HEAD_SIZE), normed_key_rows.dtype)
    key_pad = jnp.concatenate([empty_key_value, normed_key_rows], axis=0)
    value_pad = jnp.concatenate([empty_key_value, value_rows], axis=0)
    delta = jnp.sum(grad_out.astype(jnp.float32) * out_in.astype(jnp.float32), axis=-1)

    def step(carry, block):
        q_start = (block * TOK_DEV).astype(jnp.int32)
        q_blk = lax.dynamic_slice_in_dim(query, q_start, TOK_DEV, 0)
        do_blk = lax.dynamic_slice_in_dim(grad_out, q_start, TOK_DEV, 0)
        lse_blk = lax.dynamic_slice_in_dim(lse, q_start, TOK_DEV, 1)
        delta_blk = lax.dynamic_slice_in_dim(delta, q_start, TOK_DEV, 0)
        k_win = lax.dynamic_slice_in_dim(key_pad, q_start, span, 0)
        v_win = lax.dynamic_slice_in_dim(value_pad, q_start, span, 0)
        grad_q, grad_k, grad_v = band_grads(q_blk, do_blk, lse_blk, delta_blk, k_win, v_win, q_start, q_start - padding_rows)
        terms = lax.optimization_barrier(jnp.stack([grad_k, grad_v]).astype(jnp.bfloat16)).astype(carry.dtype)
        old = lax.dynamic_slice_in_dim(carry, q_start, span, 1)
        carry = lax.dynamic_update_slice_in_dim(carry, old + terms, q_start, 1)
        return carry, grad_q.astype(jnp.bfloat16)

    window_begin = jnp.zeros((2, padding_rows + SEQUENCE_TOKENS, KEY_VALUE_HEADS, HEAD_SIZE), jnp.float32)
    final, grad_blocks = lax.scan(step, window_begin, jnp.arange(N_SEQ, dtype=jnp.int32))
    grad_query = grad_blocks.reshape(SEQUENCE_TOKENS, HQ, HEAD_SIZE)
    grad_key = final[0, padding_rows:].astype(jnp.bfloat16)
    grad_value = final[1, padding_rows:].astype(jnp.bfloat16)
    return (grad_query, grad_key, grad_value)
```

```python
import functools

import jax
import jax.numpy as jnp
from jax import lax
from jax.experimental import pallas as pl
from jax.experimental.pallas import tpu as pltpu
from jax.sharding import PartitionSpec as P

WINDOW = 1024
HOPS = 8
PLANE = 4
HEADS_PER_STEP = 2

SCALE = 168.0 ** (-0.5)


def shift(x, n, distance):
    pairs = [(i, i + distance) for i in range(n) if 0 <= i + distance < n]
    return lax.ppermute(x, "seq", pairs)


def swap(x, n, bit):
    return lax.ppermute(x, "seq", [(i, i ^ bit) for i in range(n)])


def _blocks_kernel(modes, valid_ref, q_ref, do_ref, lse_ref, delta_ref, *refs):
    nb = len(modes)
    kv_refs = refs[:nb]
    dq_ref = refs[nb]
    dkv_refs = refs[nb + 1:]
    gb, grp, tok, width = q_ref.shape
    rows = grp * tok
    kk = lax.broadcasted_iota(jnp.int32, (tok, rows), 0)
    tt = lax.broadcasted_iota(jnp.int32, (tok, rows), 1) % tok
    causal = kk <= tt
    strict = kk > tt
    for g in range(gb):
        q = q_ref[g].reshape(rows, width)
        do = do_ref[g].reshape(rows, width)
        lse = lse_ref[g]
        delta = delta_ref[g]
        dq = jnp.zeros((rows, width), jnp.float32)
        for b, mode in enumerate(modes):
            k = kv_refs[b][0, g]
            v = kv_refs[b][1, g]
            off = jnp.where(valid_ref[b] > 0, 0.0, 1e30).astype(jnp.float32)
            s = lax.dot_general(k, q, (((1,), (1,)), ((), ())), preferred_element_type=jnp.float32)
            e = jnp.exp(s * SCALE - lse - off)
            if mode == 0:
                p = jnp.where(causal, e, 0.0)
            elif mode == 2:
                p = jnp.where(strict, e, 0.0)
            else:
                p = e
            dp = lax.dot_general(v, do, (((1,), (1,)), ((), ())), preferred_element_type=jnp.float32)
            ds = p * (dp - delta)
            pb = p.astype(jnp.bfloat16)
            dsb = ds.astype(jnp.bfloat16)
            dv = jnp.dot(pb, do, preferred_element_type=jnp.float32)
            dk = jnp.dot(dsb, q, preferred_element_type=jnp.float32) * SCALE
            dq = dq + lax.dot_general(dsb, k, (((0,), (0,)), ((), ())), preferred_element_type=jnp.float32)
            dkv_refs[b][0, g] = dk.astype(jnp.bfloat16)
            dkv_refs[b][1, g] = dv.astype(jnp.bfloat16)
        dq_ref[g] = (dq * SCALE).astype(dq_ref.dtype).reshape(grp, tok, width)


def attend_blocks(modes, valid, q4, do4, lse3, delta3, kvs):
    nh, grp, tok, width = q4.shape
    gb = HEADS_PER_STEP
    nb = len(modes)
    hspec = pl.BlockSpec((gb, grp, tok, width), lambda i, v: (i, 0, 0, 0))
    rspec = pl.BlockSpec((gb, 1, grp * tok), lambda i, v: (i, 0, 0))
    kvspec = pl.BlockSpec((2, gb, tok, width), lambda i, v: (0, i, 0, 0))
    out_shape = [jax.ShapeDtypeStruct(q4.shape, jnp.bfloat16)]
    out_shape += [jax.ShapeDtypeStruct(kv.shape, jnp.bfloat16) for kv in kvs]
    grid_spec = pltpu.PrefetchScalarGridSpec(
        num_scalar_prefetch=1,
        grid=(nh // gb,),
        in_specs=[hspec, hspec, rspec, rspec] + [kvspec] * nb,
        out_specs=[hspec] + [kvspec] * nb,
    )
    outs = pl.pallas_call(
        functools.partial(_blocks_kernel, tuple(modes)),
        grid_spec=grid_spec,
        out_shape=out_shape,
        compiler_params=pltpu.CompilerParams(dimension_semantics=("arbitrary",)),
    )(valid, q4, do4, lse3, delta3, *kvs)
    return outs[0], list(outs[1:])


def per_device(query, normed_key_rows, value_rows, out_in, grad_out, lse):
    tok, heads_q, width = query.shape
    heads_kv = normed_key_rows.shape[1]
    groups = heads_q // heads_kv
    n = lax.axis_size("seq")
    levels = HOPS // PLANE
    idx = lax.axis_index("seq")
    half = (idx % PLANE) // 2
    core = idx % 2

    q4 = query.transpose(1, 0, 2).reshape(heads_kv, groups, tok, width)
    do4 = grad_out.transpose(1, 0, 2).reshape(heads_kv, groups, tok, width)
    delta = jnp.sum(grad_out.astype(jnp.float32) * out_in.astype(jnp.float32), axis=-1)
    delta3 = delta.T.reshape(heads_kv, 1, groups * tok)
    lse3 = lse.reshape(heads_kv, 1, groups * tok)
    own = jnp.stack([normed_key_rows, value_rows]).transpose(0, 2, 1, 3)

    xs = [own]
    for _ in range(levels):
        xs.append(shift(xs[-1], n, PLANE))
    cs = [swap(jnp.where(core == 0, xs[k], xs[k + 1]), n, 1) for k in range(levels)]
    ys = [swap(jnp.where(half == 0, xs[0], xs[1]), n, 2)]
    for _ in range(1, levels):
        ys.append(shift(ys[-1], n, PLANE))
    ds = [swap(y, n, 1) for y in ys]

    blocks = xs + cs + ys + ds
    modes = [0] + [1] * (levels - 1) + [2] + [1] * (3 * levels)
    dist = [a * PLANE for a in range(levels + 1)]
    dist += [k * PLANE + 3 - 2 * core for k in range(levels)]
    dist += [k * PLANE + 2 for k in range(levels)]
    dist += [k * PLANE + 1 + 2 * core for k in range(levels)]
    valid = jnp.stack([(idx >= d).astype(jnp.int32) for d in dist])

    dq4, terms = attend_blocks(modes, valid, q4, do4, lse3, delta3, blocks)
    tx = terms[: levels + 1]
    tc = terms[levels + 1: 2 * levels + 1]
    ty = terms[2 * levels + 1: 3 * levels + 1]
    td = terms[3 * levels + 1:]

    f32 = jnp.float32
    bf16 = jnp.bfloat16
    ysum = [ty[k].astype(f32) + swap(td[k], n, 1).astype(f32) for k in range(levels)]
    for k in range(levels - 1, 0, -1):
        ysum[k - 1] = ysum[k - 1] + shift(ysum[k].astype(bf16), n, -PLANE).astype(f32)
    yret = swap(ysum[0].astype(bf16), n, 2).astype(f32)
    cret = [swap(tc[k], n, 1).astype(f32) for k in range(levels)]
    part = [tx[a].astype(f32) for a in range(levels + 1)]
    zero = jnp.zeros_like(part[0])
    for a in range(levels + 1):
        if a <= 1:
            part[a] = part[a] + jnp.where(half == a, yret, zero)
        for k in range(levels):
            if 0 <= a - k <= 1:
                part[a] = part[a] + jnp.where(core == a - k, cret[k], zero)
    for a in range(levels, 0, -1):
        part[a - 1] = part[a - 1] + shift(part[a].astype(bf16), n, -PLANE).astype(f32)
    grad = part[0].astype(bf16)

    grad_query = dq4.reshape(heads_q, tok, width).transpose(1, 0, 2)
    return (grad_query, grad[0].transpose(1, 0, 2), grad[1].transpose(1, 0, 2))


def solution(mesh):
    placed = (
        P(("dp", "seq"), None, None),
        P(("dp", "seq"), None, None),
        P(("dp", "seq"), None, None),
        P(("dp", "seq"), None, None),
        P(("dp", "seq"), None, None),
        P(None, ("dp", "seq")),
    )
    return jax.shard_map(
        per_device,
        mesh=mesh,
        in_specs=placed,
        out_specs=(
            P(("dp", "seq"), None, None),
            P(("dp", "seq"), None, None),
            P(("dp", "seq"), None, None),
        ),
        check_vma=False,
    )
```

```python
import functools

import jax
import jax.numpy as jnp
from jax import lax
from jax.experimental import pallas as pl
from jax.experimental.pallas import tpu as pltpu
from jax.sharding import PartitionSpec as P

WINDOW = 1024
HOPS = 8
PLANE = 4
HEADS_PER_STEP = 2

SCALE = 168.0 ** (-0.5)


def shift(x, n, distance):
    pairs = [(i, i + distance) for i in range(n) if 0 <= i + distance < n]
    return lax.ppermute(x, "seq", pairs)


def swap(x, n, bit):
    return lax.ppermute(x, "seq", [(i, i ^ bit) for i in range(n)])


def one_way(x, n, bit, side):
    pairs = [(i, i ^ bit) for i in range(n) if (i & bit) == side]
    return lax.ppermute(x, "seq", pairs)


def _blocks_kernel(modes, has_acc, valid_ref, q_ref, do_ref, lse_ref, delta_ref, *refs):
    nb = len(modes)
    if has_acc:
        acc_ref = refs[0]
        refs = refs[1:]
    kv_refs = refs[:nb]
    dq_ref = refs[nb]
    dkv_refs = refs[nb + 1:]
    gb, grp, tok, width = q_ref.shape
    rows = grp * tok
    kk = lax.broadcasted_iota(jnp.int32, (tok, rows), 0)
    tt = lax.broadcasted_iota(jnp.int32, (tok, rows), 1) % tok
    causal = kk <= tt
    strict = kk > tt
    for g in range(gb):
        q = q_ref[g].reshape(rows, width)
        do = do_ref[g].reshape(rows, width)
        lse = lse_ref[g]
        delta = delta_ref[g]
        if has_acc:
            dq = acc_ref[g].reshape(rows, width)
        else:
            dq = jnp.zeros((rows, width), jnp.float32)
        for b, mode in enumerate(modes):
            k = kv_refs[b][0, g]
            v = kv_refs[b][1, g]
            off = jnp.where(valid_ref[b] > 0, 0.0, 1e30).astype(jnp.float32)
            s = lax.dot_general(k, q, (((1,), (1,)), ((), ())), preferred_element_type=jnp.float32)
            e = jnp.exp(s * SCALE - lse - off)
            if mode == 0:
                p = jnp.where(causal, e, 0.0)
            elif mode == 2:
                p = jnp.where(strict, e, 0.0)
            else:
                p = e
            dp = lax.dot_general(v, do, (((1,), (1,)), ((), ())), preferred_element_type=jnp.float32)
            ds = p * (dp - delta)
            pb = p.astype(jnp.bfloat16)
            dsb = ds.astype(jnp.bfloat16)
            dv = jnp.dot(pb, do, preferred_element_type=jnp.float32)
            dk = jnp.dot(dsb, q, preferred_element_type=jnp.float32) * SCALE
            dq = dq + lax.dot_general(dsb, k, (((0,), (0,)), ((), ())), preferred_element_type=jnp.float32)
            dkv_refs[b][0, g] = dk.astype(jnp.bfloat16)
            dkv_refs[b][1, g] = dv.astype(jnp.bfloat16)
        dq_ref[g] = dq.reshape(grp, tok, width)


def attend_blocks(modes, dist, idx, q4, do4, lse3, delta3, acc, kvs):
    nh, grp, tok, width = q4.shape
    gb = HEADS_PER_STEP
    nb = len(modes)
    valid = jnp.stack([(idx >= d).astype(jnp.int32) for d in dist])
    hspec = pl.BlockSpec((gb, grp, tok, width), lambda i, v: (i, 0, 0, 0))
    rspec = pl.BlockSpec((gb, 1, grp * tok), lambda i, v: (i, 0, 0))
    kvspec = pl.BlockSpec((2, gb, tok, width), lambda i, v: (0, i, 0, 0))
    accs = [] if acc is None else [acc]
    out_shape = [jax.ShapeDtypeStruct(q4.shape, jnp.float32)]
    out_shape += [jax.ShapeDtypeStruct(kv.shape, jnp.bfloat16) for kv in kvs]
    grid_spec = pltpu.PrefetchScalarGridSpec(
        num_scalar_prefetch=1,
        grid=(nh // gb,),
        in_specs=[hspec, hspec, rspec, rspec] + [hspec] * len(accs) + [kvspec] * nb,
        out_specs=[hspec] + [kvspec] * nb,
    )
    outs = pl.pallas_call(
        functools.partial(_blocks_kernel, tuple(modes), acc is not None),
        grid_spec=grid_spec,
        out_shape=out_shape,
        compiler_params=pltpu.CompilerParams(dimension_semantics=("arbitrary",)),
    )(valid, q4, do4, lse3, delta3, *accs, *kvs)
    return outs[0], list(outs[1:])


def per_device(query, normed_key_rows, value_rows, out_in, grad_out, lse):
    tok, heads_q, width = query.shape
    heads_kv = normed_key_rows.shape[1]
    groups = heads_q // heads_kv
    n = lax.axis_size("seq")
    assert HOPS == 2 * PLANE
    idx = lax.axis_index("seq")
    half = (idx % PLANE) // 2
    core = idx % 2

    q4 = query.transpose(1, 0, 2).reshape(heads_kv, groups, tok, width)
    do4 = grad_out.transpose(1, 0, 2).reshape(heads_kv, groups, tok, width)
    delta = jnp.sum(grad_out.astype(jnp.float32) * out_in.astype(jnp.float32), axis=-1)
    delta3 = delta.T.reshape(heads_kv, 1, groups * tok)
    lse3 = lse.reshape(heads_kv, 1, groups * tok)
    x0 = jnp.stack([normed_key_rows, value_rows]).transpose(0, 2, 1, 3)

    x1 = shift(x0, n, PLANE)
    ya = one_way(x0, n, 2, 0)
    cx1 = swap(x1, n, 1)
    yb = one_way(x1, n, 2, 2)
    x2 = shift(x1, n, PLANE)
    ca = one_way(x0, n, 1, 0)
    cb = one_way(x2, n, 1, 1)
    y0 = jnp.where(half == 1, ya, yb)
    d0 = swap(y0, n, 1)
    y1 = shift(y0, n, PLANE)
    cxo = jnp.where(core == 1, ca, cb)
    d1 = swap(y1, n, 1)

    run = functools.partial(attend_blocks, idx=idx, q4=q4, do4=do4, lse3=lse3, delta3=delta3)
    acc, (tx0, tx1, tcx1) = run([0, 1, 1], [0, PLANE, 3 + 2 * core], acc=None, kvs=[x0, x1, cx1])
    acc, (tx2, tcxo, ty0, td0) = run(
        [2, 1, 1, 1], [2 * PLANE, 7 - 6 * core, 2, 1 + 2 * core], acc=acc, kvs=[x2, cxo, y0, d0])
    acc, (ty1, td1) = run([1, 1], [6, 5 + 2 * core], acc=acc, kvs=[y1, d1])

    f32 = jnp.float32
    bf16 = jnp.bfloat16
    r1 = swap(tcx1, n, 1).astype(f32)
    ro = swap(tcxo, n, 1).astype(f32)
    yret0 = swap((ty0.astype(f32) + swap(td0, n, 1).astype(f32)).astype(bf16), n, 2).astype(f32)
    yret1 = swap((ty1.astype(f32) + swap(td1, n, 1).astype(f32)).astype(bf16), n, 2).astype(f32)
    zero = jnp.zeros_like(r1)
    lo = half == 0
    part2 = tx2.astype(f32) + jnp.where(core == 1, ro, zero) + jnp.where(lo, zero, yret1)
    part1 = tx1.astype(f32) + r1 + jnp.where(lo, yret1, yret0)
    part1 = part1 + shift(part2.astype(bf16), n, -PLANE).astype(f32)
    part0 = tx0.astype(f32) + jnp.where(core == 0, ro, zero) + jnp.where(lo, yret0, zero)
    part0 = part0 + shift(part1.astype(bf16), n, -PLANE).astype(f32)
    grad = part0.astype(bf16)

    grad_query = (acc * SCALE).astype(bf16).reshape(heads_q, tok, width).transpose(1, 0, 2)
    return (grad_query, grad[0].transpose(1, 0, 2), grad[1].transpose(1, 0, 2))


def solution(mesh):
    placed = (
        P(("dp", "seq"), None, None),
        P(("dp", "seq"), None, None),
        P(("dp", "seq"), None, None),
        P(("dp", "seq"), None, None),
        P(("dp", "seq"), None, None),
        P(None, ("dp", "seq")),
    )
    return jax.shard_map(
        per_device,
        mesh=mesh,
        in_specs=placed,
        out_specs=(
            P(("dp", "seq"), None, None),
            P(("dp", "seq"), None, None),
            P(("dp", "seq"), None, None),
        ),
        check_vma=False,
    )
```

```python
import functools

import jax
import jax.numpy as jnp
from jax import lax
from jax.experimental import pallas as pl
from jax.experimental.pallas import tpu as pltpu
from jax.sharding import PartitionSpec as P

WINDOW = 1024
HOPS = 8
PLANE = 4
HEADS_PER_STEP = 2

SCALE = 168.0 ** (-0.5)


def shift(x, n, distance):
    pairs = [(i, i + distance) for i in range(n) if 0 <= i + distance < n]
    return lax.ppermute(x, "seq", pairs)


def swap(x, n, bit):
    return lax.ppermute(x, "seq", [(i, i ^ bit) for i in range(n)])


def one_way(x, n, bit, side):
    pairs = [(i, i ^ bit) for i in range(n) if (i & bit) == side]
    return lax.ppermute(x, "seq", pairs)


def _blocks_kernel(modes, has_acc, valid_ref, q_ref, do_ref, lse_ref, delta_ref, *refs):
    nb = len(modes)
    if has_acc:
        acc_ref = refs[0]
        refs = refs[1:]
    kv_refs = refs[:nb]
    dq_ref = refs[nb]
    dkv_refs = refs[nb + 1:]
    gb, grp, tok, width = q_ref.shape
    rows = grp * tok
    kk = lax.broadcasted_iota(jnp.int32, (tok, rows), 0)
    tt = lax.broadcasted_iota(jnp.int32, (tok, rows), 1) % tok
    causal = kk <= tt
    strict = kk > tt
    for g in range(gb):
        q = q_ref[g].reshape(rows, width)
        do = do_ref[g].reshape(rows, width)
        lse = lse_ref[g]
        delta = delta_ref[g]
        if has_acc:
            dq = acc_ref[g].reshape(rows, width)
        else:
            dq = jnp.zeros((rows, width), jnp.float32)
        for b, mode in enumerate(modes):
            k = kv_refs[b][0, g]
            v = kv_refs[b][1, g]
            off = jnp.where(valid_ref[b] > 0, 0.0, 1e30).astype(jnp.float32)
            s = lax.dot_general(k, q, (((1,), (1,)), ((), ())), preferred_element_type=jnp.float32)
            e = jnp.exp(s * SCALE - lse - off)
            if mode == 0:
                p = jnp.where(causal, e, 0.0)
            elif mode == 2:
                p = jnp.where(strict, e, 0.0)
            else:
                p = e
            dp = lax.dot_general(v, do, (((1,), (1,)), ((), ())), preferred_element_type=jnp.float32)
            ds = p * (dp - delta)
            pb = p.astype(jnp.bfloat16)
            dsb = ds.astype(jnp.bfloat16)
            dv = jnp.dot(pb, do, preferred_element_type=jnp.float32)
            dk = jnp.dot(dsb, q, preferred_element_type=jnp.float32) * SCALE
            dq = dq + lax.dot_general(dsb, k, (((0,), (0,)), ((), ())), preferred_element_type=jnp.float32)
            dkv_refs[b][0, g] = dk.astype(jnp.bfloat16)
            dkv_refs[b][1, g] = dv.astype(jnp.bfloat16)
        dq_ref[g] = dq.reshape(grp, tok, width)


def attend_blocks(modes, dist, idx, q4, do4, lse3, delta3, acc, kvs):
    nh, grp, tok, width = q4.shape
    gb = HEADS_PER_STEP
    nb = len(modes)
    valid = jnp.stack([(idx >= d).astype(jnp.int32) for d in dist])
    hspec = pl.BlockSpec((gb, grp, tok, width), lambda i, v: (i, 0, 0, 0))
    rspec = pl.BlockSpec((gb, 1, grp * tok), lambda i, v: (i, 0, 0))
    kvspec = pl.BlockSpec((2, gb, tok, width), lambda i, v: (0, i, 0, 0))
    accs = [] if acc is None else [acc]
    out_shape = [jax.ShapeDtypeStruct(q4.shape, jnp.float32)]
    out_shape += [jax.ShapeDtypeStruct(kv.shape, jnp.bfloat16) for kv in kvs]
    grid_spec = pltpu.PrefetchScalarGridSpec(
        num_scalar_prefetch=1,
        grid=(nh // gb,),
        in_specs=[hspec, hspec, rspec, rspec] + [hspec] * len(accs) + [kvspec] * nb,
        out_specs=[hspec] + [kvspec] * nb,
    )
    scores = nh * grp * tok * tok * nb
    cost = pl.CostEstimate(
        flops=10 * scores * width,
        transcendentals=scores,
        bytes_accessed=(2 + 2 * len(accs)) * q4.size * 2 + 2 * sum(kv.size for kv in kvs) * 2,
    )
    outs = pl.pallas_call(
        functools.partial(_blocks_kernel, tuple(modes), acc is not None),
        grid_spec=grid_spec,
        out_shape=out_shape,
        cost_estimate=cost,
        compiler_params=pltpu.CompilerParams(dimension_semantics=("arbitrary",)),
    )(valid, q4, do4, lse3, delta3, *accs, *kvs)
    return outs[0], list(outs[1:])


def per_device(query, normed_key_rows, value_rows, out_in, grad_out, lse):
    tok, heads_q, width = query.shape
    heads_kv = normed_key_rows.shape[1]
    groups = heads_q // heads_kv
    n = lax.axis_size("seq")
    assert HOPS == 2 * PLANE
    idx = lax.axis_index("seq")
    half = (idx % PLANE) // 2
    core = idx % 2

    q4 = query.transpose(1, 0, 2).reshape(heads_kv, groups, tok, width)
    do4 = grad_out.transpose(1, 0, 2).reshape(heads_kv, groups, tok, width)
    delta = jnp.sum(grad_out.astype(jnp.float32) * out_in.astype(jnp.float32), axis=-1)
    delta3 = delta.T.reshape(heads_kv, 1, groups * tok)
    lse3 = lse.reshape(heads_kv, 1, groups * tok)
    x0 = jnp.stack([normed_key_rows, value_rows]).transpose(0, 2, 1, 3)

    x1 = shift(x0, n, PLANE)
    ya = one_way(x0, n, 2, 0)
    cx1 = swap(x1, n, 1)
    yb = one_way(x1, n, 2, 2)
    x2 = shift(x1, n, PLANE)
    ca = one_way(x0, n, 1, 0)
    cb = one_way(x2, n, 1, 1)
    yc = one_way(x1, n, 2, 0)
    yd = one_way(x2, n, 2, 2)
    y0 = jnp.where(half == 1, ya, yb)
    d0 = swap(y0, n, 1)
    cxo = jnp.where(core == 1, ca, cb)
    y1 = jnp.where(half == 1, yc, yd)
    d1 = swap(y1, n, 1)

    run = functools.partial(attend_blocks, idx=idx, q4=q4, do4=do4, lse3=lse3, delta3=delta3)
    acc, (tx0, tx1, tcx1) = run([0, 1, 1], [0, PLANE, 3 + 2 * core], acc=None, kvs=[x0, x1, cx1])
    acc, (tx2, tcxo, ty0, td0) = run(
        [2, 1, 1, 1], [2 * PLANE, 7 - 6 * core, 2, 1 + 2 * core], acc=acc, kvs=[x2, cxo, y0, d0])
    acc, (ty1, td1) = run([1, 1], [6, 5 + 2 * core], acc=acc, kvs=[y1, d1])

    f32 = jnp.float32
    bf16 = jnp.bfloat16
    r1 = swap(tcx1, n, 1).astype(f32)
    ro = swap(tcxo, n, 1).astype(f32)
    yret0 = swap((ty0.astype(f32) + swap(td0, n, 1).astype(f32)).astype(bf16), n, 2).astype(f32)
    yret1 = swap((ty1.astype(f32) + swap(td1, n, 1).astype(f32)).astype(bf16), n, 2).astype(f32)
    zero = jnp.zeros_like(r1)
    lo = half == 0
    part2 = tx2.astype(f32) + jnp.where(core == 1, ro, zero) + jnp.where(lo, zero, yret1)
    part1 = tx1.astype(f32) + r1 + jnp.where(lo, yret1, yret0)
    part1 = part1 + shift(part2.astype(bf16), n, -PLANE).astype(f32)
    part0 = tx0.astype(f32) + jnp.where(core == 0, ro, zero) + jnp.where(lo, yret0, zero)
    part0 = part0 + shift(part1.astype(bf16), n, -PLANE).astype(f32)
    grad = part0.astype(bf16)

    grad_query = (acc * SCALE).astype(bf16).reshape(heads_q, tok, width).transpose(1, 0, 2)
    return (grad_query, grad[0].transpose(1, 0, 2), grad[1].transpose(1, 0, 2))


def solution(mesh):
    placed = (
        P(("dp", "seq"), None, None),
        P(("dp", "seq"), None, None),
        P(("dp", "seq"), None, None),
        P(("dp", "seq"), None, None),
        P(("dp", "seq"), None, None),
        P(None, ("dp", "seq")),
    )
    return jax.shard_map(
        per_device,
        mesh=mesh,
        in_specs=placed,
        out_specs=(
            P(("dp", "seq"), None, None),
            P(("dp", "seq"), None, None),
            P(("dp", "seq"), None, None),
        ),
        check_vma=False,
    )
```

```python
import functools

import jax
import jax.numpy as jnp
from jax import lax
from jax.experimental import pallas as pl
from jax.experimental.pallas import tpu as pltpu
from jax.sharding import PartitionSpec as P

WINDOW = 1024
HOPS = 8
PLANE = 4
HEADS_PER_STEP = 2

SCALE = 168.0 ** (-0.5)


def shift(x, n, distance):
    pairs = [(i, i + distance) for i in range(n) if 0 <= i + distance < n]
    return lax.ppermute(x, "seq", pairs)


def swap(x, n, bit):
    return lax.ppermute(x, "seq", [(i, i ^ bit) for i in range(n)])


def one_way(x, n, bit, side):
    pairs = [(i, i ^ bit) for i in range(n) if (i & bit) == side]
    return lax.ppermute(x, "seq", pairs)


def _blocks_kernel(modes, has_acc, valid_ref, q_ref, do_ref, lse_ref, delta_ref, *refs):
    nb = len(modes)
    if has_acc:
        acc_ref = refs[0]
        refs = refs[1:]
    kv_refs = refs[:nb]
    dq_ref = refs[nb]
    dkv_refs = refs[nb + 1:]
    gb, grp, tok, width = q_ref.shape
    rows = grp * tok
    kk = lax.broadcasted_iota(jnp.int32, (tok, rows), 0)
    tt = lax.broadcasted_iota(jnp.int32, (tok, rows), 1) % tok
    causal = kk <= tt
    strict = kk > tt
    for g in range(gb):
        q = q_ref[g].reshape(rows, width)
        do = do_ref[g].reshape(rows, width)
        lse = lse_ref[g]
        delta = delta_ref[g]
        if has_acc:
            dq = acc_ref[g].reshape(rows, width)
        else:
            dq = jnp.zeros((rows, width), jnp.float32)
        for b, mode in enumerate(modes):
            k = kv_refs[b][0, g]
            v = kv_refs[b][1, g]
            off = jnp.where(valid_ref[b] > 0, 0.0, 1e30).astype(jnp.float32)
            s = lax.dot_general(k, q, (((1,), (1,)), ((), ())), preferred_element_type=jnp.float32)
            e = jnp.exp(s * SCALE - lse - off)
            if mode == 0:
                p = jnp.where(causal, e, 0.0)
            elif mode == 2:
                p = jnp.where(strict, e, 0.0)
            else:
                p = e
            dp = lax.dot_general(v, do, (((1,), (1,)), ((), ())), preferred_element_type=jnp.float32)
            ds = p * (dp - delta)
            pb = p.astype(jnp.bfloat16)
            dsb = ds.astype(jnp.bfloat16)
            dv = jnp.dot(pb, do, preferred_element_type=jnp.float32)
            dk = jnp.dot(dsb, q, preferred_element_type=jnp.float32) * SCALE
            dq = dq + lax.dot_general(dsb, k, (((0,), (0,)), ((), ())), preferred_element_type=jnp.float32)
            dkv_refs[b][0, g] = dk.astype(jnp.bfloat16)
            dkv_refs[b][1, g] = dv.astype(jnp.bfloat16)
        dq_ref[g] = dq.reshape(grp, tok, width)


def attend_blocks(modes, dist, idx, q4, do4, lse3, delta3, acc, kvs):
    nh, grp, tok, width = q4.shape
    gb = HEADS_PER_STEP
    nb = len(modes)
    valid = jnp.stack([(idx >= d).astype(jnp.int32) for d in dist])
    hspec = pl.BlockSpec((gb, grp, tok, width), lambda i, v: (i, 0, 0, 0))
    rspec = pl.BlockSpec((gb, 1, grp * tok), lambda i, v: (i, 0, 0))
    kvspec = pl.BlockSpec((2, gb, tok, width), lambda i, v: (0, i, 0, 0))
    accs = [] if acc is None else [acc]
    out_shape = [jax.ShapeDtypeStruct(q4.shape, jnp.float32)]
    out_shape += [jax.ShapeDtypeStruct(kv.shape, jnp.bfloat16) for kv in kvs]
    grid_spec = pltpu.PrefetchScalarGridSpec(
        num_scalar_prefetch=1,
        grid=(nh // gb,),
        in_specs=[hspec, hspec, rspec, rspec] + [hspec] * len(accs) + [kvspec] * nb,
        out_specs=[hspec] + [kvspec] * nb,
    )
    scores = nh * grp * tok * tok * nb
    cost = pl.CostEstimate(
        flops=10 * scores * width,
        transcendentals=scores,
        bytes_accessed=(2 + 2 * len(accs)) * q4.size * 2 + 2 * sum(kv.size for kv in kvs) * 2,
    )
    outs = pl.pallas_call(
        functools.partial(_blocks_kernel, tuple(modes), acc is not None),
        grid_spec=grid_spec,
        out_shape=out_shape,
        cost_estimate=cost,
        compiler_params=pltpu.CompilerParams(dimension_semantics=("arbitrary",)),
    )(valid, q4, do4, lse3, delta3, *accs, *kvs)
    return outs[0], list(outs[1:])


def per_device(query, normed_key_rows, value_rows, out_in, grad_out, lse):
    tok, heads_q, width = query.shape
    heads_kv = normed_key_rows.shape[1]
    groups = heads_q // heads_kv
    n = lax.axis_size("seq")
    assert HOPS == 2 * PLANE
    idx = lax.axis_index("seq")
    half = (idx % PLANE) // 2
    core = idx % 2

    q4 = query.transpose(1, 0, 2).reshape(heads_kv, groups, tok, width)
    do4 = grad_out.transpose(1, 0, 2).reshape(heads_kv, groups, tok, width)
    delta = jnp.sum(grad_out.astype(jnp.float32) * out_in.astype(jnp.float32), axis=-1)
    delta3 = delta.T.reshape(heads_kv, 1, groups * tok)
    lse3 = lse.reshape(heads_kv, 1, groups * tok)
    x0 = jnp.stack([normed_key_rows, value_rows]).transpose(0, 2, 1, 3)

    x1 = shift(x0, n, PLANE)
    ya = one_way(x0, n, 2, 0)
    cx1 = swap(x1, n, 1)
    yb = one_way(x1, n, 2, 2)
    x2 = shift(x1, n, PLANE)
    ca = one_way(x0, n, 1, 0)
    cb = one_way(x2, n, 1, 1)
    yc = one_way(x1, n, 2, 0)
    yd = one_way(x2, n, 2, 2)
    y0 = jnp.where(half == 1, ya, yb)
    d0 = swap(y0, n, 1)
    cxo = jnp.where(core == 1, ca, cb)
    y1 = jnp.where(half == 1, yc, yd)
    d1 = swap(y1, n, 1)

    acc, terms = attend_blocks(
        [0, 1, 1, 2, 1, 1, 1, 1, 1],
        [0, PLANE, 3 + 2 * core, 2 * PLANE, 7 - 6 * core, 2, 1 + 2 * core, 6, 5 + 2 * core],
        idx, q4, do4, lse3, delta3, None, [x0, x1, cx1, x2, cxo, y0, d0, y1, d1])
    tx0, tx1, tcx1, tx2, tcxo, ty0, td0, ty1, td1 = terms

    f32 = jnp.float32
    bf16 = jnp.bfloat16
    r1 = swap(tcx1, n, 1).astype(f32)
    ro = swap(tcxo, n, 1).astype(f32)
    yret0 = swap((ty0.astype(f32) + swap(td0, n, 1).astype(f32)).astype(bf16), n, 2).astype(f32)
    yret1 = swap((ty1.astype(f32) + swap(td1, n, 1).astype(f32)).astype(bf16), n, 2).astype(f32)
    zero = jnp.zeros_like(r1)
    lo = half == 0
    part2 = tx2.astype(f32) + jnp.where(core == 1, ro, zero) + jnp.where(lo, zero, yret1)
    part1 = tx1.astype(f32) + r1 + jnp.where(lo, yret1, yret0)
    part1 = part1 + shift(part2.astype(bf16), n, -PLANE).astype(f32)
    part0 = tx0.astype(f32) + jnp.where(core == 0, ro, zero) + jnp.where(lo, yret0, zero)
    part0 = part0 + shift(part1.astype(bf16), n, -PLANE).astype(f32)
    grad = part0.astype(bf16)

    grad_query = (acc * SCALE).astype(bf16).reshape(heads_q, tok, width).transpose(1, 0, 2)
    return (grad_query, grad[0].transpose(1, 0, 2), grad[1].transpose(1, 0, 2))


def solution(mesh):
    placed = (
        P(("dp", "seq"), None, None),
        P(("dp", "seq"), None, None),
        P(("dp", "seq"), None, None),
        P(("dp", "seq"), None, None),
        P(("dp", "seq"), None, None),
        P(None, ("dp", "seq")),
    )
    return jax.shard_map(
        per_device,
        mesh=mesh,
        in_specs=placed,
        out_specs=(
            P(("dp", "seq"), None, None),
            P(("dp", "seq"), None, None),
            P(("dp", "seq"), None, None),
        ),
        check_vma=False,
    )
```

```python
import functools

import jax
import jax.numpy as jnp
from jax import lax
from jax.experimental import pallas as pl
from jax.experimental.pallas import tpu as pltpu
from jax.sharding import PartitionSpec as P

WINDOW = 1024
HOPS = 8
PLANE = 4
HEADS_PER_STEP = 2

SCALE = 168.0 ** (-0.5)


def shift(x, n, distance):
    pairs = [(i, i + distance) for i in range(n) if 0 <= i + distance < n]
    return lax.ppermute(x, "seq", pairs)


def swap(x, n, bit):
    return lax.ppermute(x, "seq", [(i, i ^ bit) for i in range(n)])


def one_way(x, n, bit, side):
    pairs = [(i, i ^ bit) for i in range(n) if (i & bit) == side]
    return lax.ppermute(x, "seq", pairs)


def _blocks_kernel(modes, has_acc, valid_ref, q_ref, do_ref, lse_ref, delta_ref, *refs):
    nb = len(modes)
    if has_acc:
        acc_ref = refs[0]
        refs = refs[1:]
    k_refs = refs[:nb]
    v_refs = refs[nb:2 * nb]
    dq_ref = refs[2 * nb]
    dk_refs = refs[2 * nb + 1:3 * nb + 1]
    dv_refs = refs[3 * nb + 1:]
    gb, grp, tok, width = q_ref.shape
    rows = grp * tok
    kk = lax.broadcasted_iota(jnp.int32, (tok, rows), 0)
    tt = lax.broadcasted_iota(jnp.int32, (tok, rows), 1) % tok
    causal = kk <= tt
    strict = kk > tt
    for g in range(gb):
        q = q_ref[g].reshape(rows, width)
        do = do_ref[g].reshape(rows, width)
        lse = lse_ref[g]
        delta = delta_ref[g]
        if has_acc:
            dq = acc_ref[g].reshape(rows, width)
        else:
            dq = jnp.zeros((rows, width), jnp.float32)
        for b, mode in enumerate(modes):
            k = k_refs[b][0, g]
            v = v_refs[b][0, g]
            off = jnp.where(valid_ref[b] > 0, 0.0, 1e30).astype(jnp.float32)
            s = lax.dot_general(k, q, (((1,), (1,)), ((), ())), preferred_element_type=jnp.float32)
            e = jnp.exp(s * SCALE - lse - off)
            if mode == 0:
                p = jnp.where(causal, e, 0.0)
            elif mode == 2:
                p = jnp.where(strict, e, 0.0)
            else:
                p = e
            dp = lax.dot_general(v, do, (((1,), (1,)), ((), ())), preferred_element_type=jnp.float32)
            ds = p * (dp - delta)
            pb = p.astype(jnp.bfloat16)
            dsb = ds.astype(jnp.bfloat16)
            dv = jnp.dot(pb, do, preferred_element_type=jnp.float32)
            dk = jnp.dot(dsb, q, preferred_element_type=jnp.float32) * SCALE
            dq = dq + lax.dot_general(dsb, k, (((0,), (0,)), ((), ())), preferred_element_type=jnp.float32)
            dk_refs[b][0, g] = dk.astype(jnp.bfloat16)
            dv_refs[b][0, g] = dv.astype(jnp.bfloat16)
        dq_ref[g] = dq.reshape(grp, tok, width)


def attend_blocks(modes, dist, idx, q4, do4, lse3, delta3, acc, kvs):
    nh, grp, tok, width = q4.shape
    gb = HEADS_PER_STEP
    nb = len(modes)
    valid = jnp.stack([(idx >= d).astype(jnp.int32) for d in dist])
    hspec = pl.BlockSpec((gb, grp, tok, width), lambda i, v: (i, 0, 0, 0))
    rspec = pl.BlockSpec((gb, 1, grp * tok), lambda i, v: (i, 0, 0))
    kvspec = pl.BlockSpec((1, gb, tok, width), lambda i, v: (0, i, 0, 0))
    accs = [] if acc is None else [acc]
    out_shape = [jax.ShapeDtypeStruct(q4.shape, jnp.float32)]
    out_shape += [jax.ShapeDtypeStruct(kv.shape, jnp.bfloat16) for kv in kvs]
    grid_spec = pltpu.PrefetchScalarGridSpec(
        num_scalar_prefetch=1,
        grid=(nh // gb,),
        in_specs=[hspec, hspec, rspec, rspec] + [hspec] * len(accs) + [kvspec] * (2 * nb),
        out_specs=[hspec] + [kvspec] * (2 * nb),
    )
    scores = nh * grp * tok * tok * nb
    cost = pl.CostEstimate(
        flops=10 * scores * width,
        transcendentals=scores,
        bytes_accessed=(2 + 2 * len(accs)) * q4.size * 2 + 2 * sum(kv.size for kv in kvs) * 2,
    )
    outs = pl.pallas_call(
        functools.partial(_blocks_kernel, tuple(modes), acc is not None),
        grid_spec=grid_spec,
        out_shape=out_shape,
        cost_estimate=cost,
        compiler_params=pltpu.CompilerParams(dimension_semantics=("arbitrary",)),
    )(valid, q4, do4, lse3, delta3, *accs, *kvs)
    return outs[0], list(outs[1:])


def route(x0, n, half, core):
    x1 = shift(x0, n, PLANE)
    ya = one_way(x0, n, 2, 0)
    cx1 = swap(x1, n, 1)
    yb = one_way(x1, n, 2, 2)
    x2 = shift(x1, n, PLANE)
    ca = one_way(x0, n, 1, 0)
    cb = one_way(x2, n, 1, 1)
    yc = one_way(x1, n, 2, 0)
    yd = one_way(x2, n, 2, 2)
    y0 = jnp.where(half == 1, ya, yb)
    d0 = swap(y0, n, 1)
    cxo = jnp.where(core == 1, ca, cb)
    y1 = jnp.where(half == 1, yc, yd)
    d1 = swap(y1, n, 1)
    return [x0, x1, cx1, x2, cxo, y0, d0, y1, d1]


def unroute(terms, n, half, core):
    tx0, tx1, tcx1, tx2, tcxo, ty0, td0, ty1, td1 = terms
    f32 = jnp.float32
    bf16 = jnp.bfloat16
    r1 = swap(tcx1, n, 1).astype(f32)
    ro = swap(tcxo, n, 1).astype(f32)
    yret0 = swap((ty0.astype(f32) + swap(td0, n, 1).astype(f32)).astype(bf16), n, 2).astype(f32)
    yret1 = swap((ty1.astype(f32) + swap(td1, n, 1).astype(f32)).astype(bf16), n, 2).astype(f32)
    zero = jnp.zeros_like(r1)
    lo = half == 0
    part2 = tx2.astype(f32) + jnp.where(core == 1, ro, zero) + jnp.where(lo, zero, yret1)
    part1 = tx1.astype(f32) + r1 + jnp.where(lo, yret1, yret0)
    part1 = part1 + shift(part2.astype(bf16), n, -PLANE).astype(f32)
    part0 = tx0.astype(f32) + jnp.where(core == 0, ro, zero) + jnp.where(lo, yret0, zero)
    part0 = part0 + shift(part1.astype(bf16), n, -PLANE).astype(f32)
    return part0.astype(bf16)


def per_device(query, normed_key_rows, value_rows, out_in, grad_out, lse):
    tok, heads_q, width = query.shape
    heads_kv = normed_key_rows.shape[1]
    groups = heads_q // heads_kv
    n = lax.axis_size("seq")
    assert HOPS == 2 * PLANE
    idx = lax.axis_index("seq")
    half = (idx % PLANE) // 2
    core = idx % 2

    q4 = query.transpose(1, 0, 2).reshape(heads_kv, groups, tok, width)
    do4 = grad_out.transpose(1, 0, 2).reshape(heads_kv, groups, tok, width)
    delta = jnp.sum(grad_out.astype(jnp.float32) * out_in.astype(jnp.float32), axis=-1)
    delta3 = delta.T.reshape(heads_kv, 1, groups * tok)
    lse3 = lse.reshape(heads_kv, 1, groups * tok)
    kb = route(normed_key_rows.transpose(1, 0, 2)[None], n, half, core)
    vb = route(value_rows.transpose(1, 0, 2)[None], n, half, core)

    acc, terms = attend_blocks(
        [0, 1, 1, 2, 1, 1, 1, 1, 1],
        [0, PLANE, 3 + 2 * core, 2 * PLANE, 7 - 6 * core, 2, 1 + 2 * core, 6, 5 + 2 * core],
        idx, q4, do4, lse3, delta3, None, kb + vb)
    grad_k = unroute(terms[:9], n, half, core)
    grad_v = unroute(terms[9:], n, half, core)

    grad_query = (acc * SCALE).astype(jnp.bfloat16).reshape(heads_q, tok, width).transpose(1, 0, 2)
    return (grad_query, grad_k[0].transpose(1, 0, 2), grad_v[0].transpose(1, 0, 2))


def solution(mesh):
    placed = (
        P(("dp", "seq"), None, None),
        P(("dp", "seq"), None, None),
        P(("dp", "seq"), None, None),
        P(("dp", "seq"), None, None),
        P(("dp", "seq"), None, None),
        P(None, ("dp", "seq")),
    )
    return jax.shard_map(
        per_device,
        mesh=mesh,
        in_specs=placed,
        out_specs=(
            P(("dp", "seq"), None, None),
            P(("dp", "seq"), None, None),
            P(("dp", "seq"), None, None),
        ),
        check_vma=False,
    )
```

```python
import functools

import jax
import jax.numpy as jnp
from jax import lax
from jax.experimental import pallas as pl
from jax.experimental.pallas import tpu as pltpu
from jax.sharding import PartitionSpec as P

WINDOW = 1024
HOPS = 8
PLANE = 4
HEADS_PER_STEP = 2

SCALE = 168.0 ** (-0.5)


def shift(x, n, distance):
    pairs = [(i, i + distance) for i in range(n) if 0 <= i + distance < n]
    return lax.ppermute(x, "seq", pairs)


def swap(x, n, bit):
    return lax.ppermute(x, "seq", [(i, i ^ bit) for i in range(n)])


def one_way(x, n, bit, side):
    pairs = [(i, i ^ bit) for i in range(n) if (i & bit) == side]
    return lax.ppermute(x, "seq", pairs)


def _blocks_kernel(modes, has_acc, valid_ref, q_ref, do_ref, lse_ref, delta_ref, *refs):
    nb = len(modes)
    if has_acc:
        acc_ref = refs[0]
        refs = refs[1:]
    k_refs = refs[:nb]
    v_refs = refs[nb:2 * nb]
    dq_ref = refs[2 * nb]
    dk_refs = refs[2 * nb + 1:3 * nb + 1]
    dv_refs = refs[3 * nb + 1:]
    gb, grp, tok, width = q_ref.shape
    rows = grp * tok
    kk = lax.broadcasted_iota(jnp.int32, (tok, rows), 0)
    tt = lax.broadcasted_iota(jnp.int32, (tok, rows), 1) % tok
    causal = kk <= tt
    strict = kk > tt
    for g in range(gb):
        q = q_ref[g].reshape(rows, width)
        do = do_ref[g].reshape(rows, width)
        lse = lse_ref[g]
        delta = delta_ref[g]
        if has_acc:
            dq = acc_ref[g]
        else:
            dq = jnp.zeros((width, rows), jnp.float32)
        for b, mode in enumerate(modes):
            k = k_refs[b][0, g]
            v = v_refs[b][0, g]
            off = jnp.where(valid_ref[b] > 0, 0.0, 1e30).astype(jnp.float32)
            s = lax.dot_general(k, q, (((1,), (1,)), ((), ())), preferred_element_type=jnp.float32)
            e = jnp.exp(s * SCALE - lse - off)
            if mode == 0:
                p = jnp.where(causal, e, 0.0)
            elif mode == 2:
                p = jnp.where(strict, e, 0.0)
            else:
                p = e
            dp = lax.dot_general(v, do, (((1,), (1,)), ((), ())), preferred_element_type=jnp.float32)
            ds = p * (dp - delta)
            pb = p.astype(jnp.bfloat16)
            dsb = ds.astype(jnp.bfloat16)
            dv = jnp.dot(pb, do, preferred_element_type=jnp.float32)
            dk = jnp.dot(dsb, q, preferred_element_type=jnp.float32) * SCALE
            dq = dq + lax.dot_general(k, dsb, (((0,), (0,)), ((), ())), preferred_element_type=jnp.float32)
            dk_refs[b][0, g] = dk.astype(jnp.bfloat16)
            dv_refs[b][0, g] = dv.astype(jnp.bfloat16)
        dq_ref[g] = dq


def attend_blocks(modes, dist, idx, q4, do4, lse3, delta3, acc, kvs):
    nh, grp, tok, width = q4.shape
    gb = HEADS_PER_STEP
    nb = len(modes)
    valid = jnp.stack([(idx >= d).astype(jnp.int32) for d in dist])
    hspec = pl.BlockSpec((gb, grp, tok, width), lambda i, v: (i, 0, 0, 0))
    tspec = pl.BlockSpec((gb, width, grp * tok), lambda i, v: (i, 0, 0))
    rspec = pl.BlockSpec((gb, 1, grp * tok), lambda i, v: (i, 0, 0))
    kvspec = pl.BlockSpec((1, gb, tok, width), lambda i, v: (0, i, 0, 0))
    accs = [] if acc is None else [acc]
    out_shape = [jax.ShapeDtypeStruct((nh, width, grp * tok), jnp.float32)]
    out_shape += [jax.ShapeDtypeStruct(kv.shape, jnp.bfloat16) for kv in kvs]
    grid_spec = pltpu.PrefetchScalarGridSpec(
        num_scalar_prefetch=1,
        grid=(nh // gb,),
        in_specs=[hspec, hspec, rspec, rspec] + [tspec] * len(accs) + [kvspec] * (2 * nb),
        out_specs=[tspec] + [kvspec] * (2 * nb),
    )
    scores = nh * grp * tok * tok * nb
    cost = pl.CostEstimate(
        flops=10 * scores * width,
        transcendentals=scores,
        bytes_accessed=(2 + 2 * len(accs)) * q4.size * 2 + 2 * sum(kv.size for kv in kvs) * 2,
    )
    outs = pl.pallas_call(
        functools.partial(_blocks_kernel, tuple(modes), acc is not None),
        grid_spec=grid_spec,
        out_shape=out_shape,
        cost_estimate=cost,
        compiler_params=pltpu.CompilerParams(dimension_semantics=("arbitrary",)),
    )(valid, q4, do4, lse3, delta3, *accs, *kvs)
    return outs[0], list(outs[1:])


def route(x0, n, half, core):
    x1 = shift(x0, n, PLANE)
    ya = one_way(x0, n, 2, 0)
    cx1 = swap(x1, n, 1)
    yb = one_way(x1, n, 2, 2)
    x2 = shift(x1, n, PLANE)
    ca = one_way(x0, n, 1, 0)
    cb = one_way(x2, n, 1, 1)
    yc = one_way(x1, n, 2, 0)
    yd = one_way(x2, n, 2, 2)
    y0 = jnp.where(half == 1, ya, yb)
    d0 = swap(y0, n, 1)
    cxo = jnp.where(core == 1, ca, cb)
    y1 = jnp.where(half == 1, yc, yd)
    d1 = swap(y1, n, 1)
    return [x0, x1, cx1, x2, cxo, y0, d0, y1, d1]


def unroute(terms, n, half, core):
    tx0, tx1, tcx1, tx2, tcxo, ty0, td0, ty1, td1 = terms
    f32 = jnp.float32
    bf16 = jnp.bfloat16
    r1 = swap(tcx1, n, 1).astype(f32)
    ro = swap(tcxo, n, 1).astype(f32)
    yret0 = swap((ty0.astype(f32) + swap(td0, n, 1).astype(f32)).astype(bf16), n, 2).astype(f32)
    yret1 = swap((ty1.astype(f32) + swap(td1, n, 1).astype(f32)).astype(bf16), n, 2).astype(f32)
    zero = jnp.zeros_like(r1)
    lo = half == 0
    part2 = tx2.astype(f32) + jnp.where(core == 1, ro, zero) + jnp.where(lo, zero, yret1)
    part1 = tx1.astype(f32) + r1 + jnp.where(lo, yret1, yret0)
    part1 = part1 + shift(part2.astype(bf16), n, -PLANE).astype(f32)
    part0 = tx0.astype(f32) + jnp.where(core == 0, ro, zero) + jnp.where(lo, yret0, zero)
    part0 = part0 + shift(part1.astype(bf16), n, -PLANE).astype(f32)
    return part0.astype(bf16)


def per_device(query, normed_key_rows, value_rows, out_in, grad_out, lse):
    tok, heads_q, width = query.shape
    heads_kv = normed_key_rows.shape[1]
    groups = heads_q // heads_kv
    n = lax.axis_size("seq")
    assert HOPS == 2 * PLANE
    idx = lax.axis_index("seq")
    half = (idx % PLANE) // 2
    core = idx % 2

    q4 = query.transpose(1, 0, 2).reshape(heads_kv, groups, tok, width)
    do4 = grad_out.transpose(1, 0, 2).reshape(heads_kv, groups, tok, width)
    delta = jnp.sum(grad_out.astype(jnp.float32) * out_in.astype(jnp.float32), axis=-1)
    delta3 = delta.T.reshape(heads_kv, 1, groups * tok)
    lse3 = lse.reshape(heads_kv, 1, groups * tok)
    kb = route(normed_key_rows.transpose(1, 0, 2)[None], n, half, core)
    vb = route(value_rows.transpose(1, 0, 2)[None], n, half, core)

    acc, terms = attend_blocks(
        [0, 1, 1, 2, 1, 1, 1, 1, 1],
        [0, PLANE, 3 + 2 * core, 2 * PLANE, 7 - 6 * core, 2, 1 + 2 * core, 6, 5 + 2 * core],
        idx, q4, do4, lse3, delta3, None, kb + vb)
    grad_k = unroute(terms[:9], n, half, core)
    grad_v = unroute(terms[9:], n, half, core)

    dq = (acc * SCALE).astype(jnp.bfloat16).reshape(heads_kv, width, groups, tok)
    grad_query = dq.transpose(3, 0, 2, 1).reshape(tok, heads_q, width)
    return (grad_query, grad_k[0].transpose(1, 0, 2), grad_v[0].transpose(1, 0, 2))


def solution(mesh):
    placed = (
        P(("dp", "seq"), None, None),
        P(("dp", "seq"), None, None),
        P(("dp", "seq"), None, None),
        P(("dp", "seq"), None, None),
        P(("dp", "seq"), None, None),
        P(None, ("dp", "seq")),
    )
    return jax.shard_map(
        per_device,
        mesh=mesh,
        in_specs=placed,
        out_specs=(
            P(("dp", "seq"), None, None),
            P(("dp", "seq"), None, None),
            P(("dp", "seq"), None, None),
        ),
        check_vma=False,
    )
```

```python
import functools

import jax
import jax.numpy as jnp
from jax import lax
from jax.experimental import pallas as pl
from jax.experimental.pallas import tpu as pltpu
from jax.sharding import PartitionSpec as P

WINDOW = 1024
HOPS = 8
PLANE = 4
HEADS_PER_STEP = 2

SCALE = 168.0 ** (-0.5)


def shift(x, n, distance):
    pairs = [(i, i + distance) for i in range(n) if 0 <= i + distance < n]
    return lax.ppermute(x, "seq", pairs)


def swap(x, n, bit):
    return lax.ppermute(x, "seq", [(i, i ^ bit) for i in range(n)])


def one_way(x, n, bit, side):
    pairs = [(i, i ^ bit) for i in range(n) if (i & bit) == side]
    return lax.ppermute(x, "seq", pairs)


def _blocks_kernel(modes, has_acc, valid_ref, q_ref, do_ref, lse_ref, delta_ref, *refs):
    nb = len(modes)
    if has_acc:
        acc_ref = refs[0]
        refs = refs[1:]
    k_refs = refs[:nb]
    v_refs = refs[nb:2 * nb]
    dq_ref = refs[2 * nb]
    dk_refs = refs[2 * nb + 1:3 * nb + 1]
    dv_refs = refs[3 * nb + 1:]
    gb, grp, tok, width = q_ref.shape
    rows = grp * tok
    kk = lax.broadcasted_iota(jnp.int32, (tok, rows), 0)
    tt = lax.broadcasted_iota(jnp.int32, (tok, rows), 1) % tok
    causal = kk <= tt
    strict = kk > tt
    for g in range(gb):
        q = q_ref[g].reshape(rows, width)
        do = do_ref[g].reshape(rows, width)
        lse = lse_ref[g]
        delta = delta_ref[g]
        if has_acc:
            dq = acc_ref[g]
        else:
            dq = jnp.zeros((width, rows), jnp.float32)
        for b, mode in enumerate(modes):
            k = k_refs[b][0, g]
            v = v_refs[b][0, g]
            off = jnp.where(valid_ref[b] > 0, 0.0, 1e30).astype(jnp.float32)
            s = lax.dot_general(k, q, (((1,), (1,)), ((), ())), preferred_element_type=jnp.float32)
            e = jnp.exp(s * SCALE - lse - off)
            if mode == 0:
                p = jnp.where(causal, e, 0.0)
            elif mode == 2:
                p = jnp.where(strict, e, 0.0)
            else:
                p = e
            dp = lax.dot_general(v, do, (((1,), (1,)), ((), ())), preferred_element_type=jnp.float32)
            ds = p * (dp - delta)
            pb = p.astype(jnp.bfloat16)
            dsb = ds.astype(jnp.bfloat16)
            dv = jnp.dot(pb, do, preferred_element_type=jnp.float32)
            dk = jnp.dot(dsb, q, preferred_element_type=jnp.float32) * SCALE
            dq = dq + lax.dot_general(k, dsb, (((0,), (0,)), ((), ())), preferred_element_type=jnp.float32)
            dk_refs[b][0, g] = dk.astype(jnp.bfloat16)
            dv_refs[b][0, g] = dv.astype(jnp.bfloat16)
        dq_ref[g] = dq


def attend_blocks(modes, dist, idx, q4, do4, lse3, delta3, acc, kvs):
    nh, grp, tok, width = q4.shape
    gb = HEADS_PER_STEP
    nb = len(modes)
    valid = jnp.stack([(idx >= d).astype(jnp.int32) for d in dist])
    hspec = pl.BlockSpec((gb, grp, tok, width), lambda i, v: (i, 0, 0, 0))
    tspec = pl.BlockSpec((gb, width, grp * tok), lambda i, v: (i, 0, 0))
    rspec = pl.BlockSpec((gb, 1, grp * tok), lambda i, v: (i, 0, 0))
    kvspec = pl.BlockSpec((1, gb, tok, width), lambda i, v: (0, i, 0, 0))
    accs = [] if acc is None else [acc]
    out_shape = [jax.ShapeDtypeStruct((nh, width, grp * tok), jnp.float32)]
    out_shape += [jax.ShapeDtypeStruct(kv.shape, jnp.bfloat16) for kv in kvs]
    grid_spec = pltpu.PrefetchScalarGridSpec(
        num_scalar_prefetch=1,
        grid=(nh // gb,),
        in_specs=[hspec, hspec, rspec, rspec] + [tspec] * len(accs) + [kvspec] * (2 * nb),
        out_specs=[tspec] + [kvspec] * (2 * nb),
    )
    scores = nh * grp * tok * tok * nb
    cost = pl.CostEstimate(
        flops=10 * scores * width,
        transcendentals=scores,
        bytes_accessed=(2 + 2 * len(accs)) * q4.size * 2 + 2 * sum(kv.size for kv in kvs) * 2,
    )
    outs = pl.pallas_call(
        functools.partial(_blocks_kernel, tuple(modes), acc is not None),
        grid_spec=grid_spec,
        out_shape=out_shape,
        cost_estimate=cost,
        compiler_params=pltpu.CompilerParams(dimension_semantics=("arbitrary",)),
    )(valid, q4, do4, lse3, delta3, *accs, *kvs)
    return outs[0], list(outs[1:])


def route(x0, n, half, core):
    x1 = shift(x0, n, PLANE)
    ya = one_way(x0, n, 2, 0)
    cx1 = swap(x1, n, 1)
    yb = one_way(x1, n, 2, 2)
    x2 = shift(x1, n, PLANE)
    ca = one_way(x0, n, 1, 0)
    cb = one_way(x2, n, 1, 1)
    yc = one_way(x1, n, 2, 0)
    yd = one_way(x2, n, 2, 2)
    y0 = jnp.where(half == 1, ya, yb)
    d0 = swap(y0, n, 1)
    cxo = jnp.where(core == 1, ca, cb)
    y1 = jnp.where(half == 1, yc, yd)
    d1 = swap(y1, n, 1)
    return [x0, x1, cx1, x2, cxo, y0, d0, y1, d1]


def gather_y(terms, n):
    tx0, tx1, tcx1, tx2, tcxo, ty0, td0, ty1, td1 = terms
    f32 = jnp.float32
    bf16 = jnp.bfloat16
    ys0 = (ty0.astype(f32) + swap(td0, n, 1).astype(f32)).astype(bf16)
    ys1 = (ty1.astype(f32) + swap(td1, n, 1).astype(f32)).astype(bf16)
    return ys0, ys1


def unroute(terms, ys0, ys1, n, half, core):
    tx0, tx1, tcx1, tx2, tcxo, ty0, td0, ty1, td1 = terms
    f32 = jnp.float32
    bf16 = jnp.bfloat16
    yret0 = swap(ys0, n, 2).astype(f32)
    yret1 = swap(ys1, n, 2).astype(f32)
    ro = swap(tcxo, n, 1).astype(f32)
    r1 = swap(tcx1, n, 1).astype(f32)
    zero = jnp.zeros_like(r1)
    lo = half == 0
    part2 = tx2.astype(f32) + jnp.where(core == 1, ro, zero) + jnp.where(lo, zero, yret1)
    part1 = tx1.astype(f32) + r1 + jnp.where(lo, yret1, yret0)
    part1 = part1 + shift(part2.astype(bf16), n, -PLANE).astype(f32)
    part0 = tx0.astype(f32) + jnp.where(core == 0, ro, zero) + jnp.where(lo, yret0, zero)
    part0 = part0 + shift(part1.astype(bf16), n, -PLANE).astype(f32)
    return part0.astype(bf16)


def per_device(query, normed_key_rows, value_rows, out_in, grad_out, lse):
    tok, heads_q, width = query.shape
    heads_kv = normed_key_rows.shape[1]
    groups = heads_q // heads_kv
    n = lax.axis_size("seq")
    assert HOPS == 2 * PLANE
    idx = lax.axis_index("seq")
    half = (idx % PLANE) // 2
    core = idx % 2

    q4 = query.transpose(1, 0, 2).reshape(heads_kv, groups, tok, width)
    do4 = grad_out.transpose(1, 0, 2).reshape(heads_kv, groups, tok, width)
    delta = jnp.sum(grad_out.astype(jnp.float32) * out_in.astype(jnp.float32), axis=-1)
    delta3 = delta.T.reshape(heads_kv, 1, groups * tok)
    lse3 = lse.reshape(heads_kv, 1, groups * tok)
    kb = route(normed_key_rows.transpose(1, 0, 2)[None], n, half, core)
    vb = route(value_rows.transpose(1, 0, 2)[None], n, half, core)

    late = [3, 4, 5, 6, 7, 8]
    early = [0, 1, 2]
    modes = [0, 1, 1, 2, 1, 1, 1, 1, 1]
    dist = [0, PLANE, 3 + 2 * core, 2 * PLANE, 7 - 6 * core, 2, 1 + 2 * core, 6, 5 + 2 * core]
    terms = [None] * 18
    acc = None
    ys = None
    qb = q4
    for sel in (late, early):
        acc, out = attend_blocks(
            [modes[j] for j in sel], [dist[j] for j in sel], idx, qb, do4, lse3, delta3, acc,
            [kb[j] for j in sel] + [vb[j] for j in sel])
        for m, j in enumerate(sel):
            terms[j] = out[m]
            terms[9 + j] = out[len(sel) + m]
        if ys is None:
            ys = gather_y(terms[:9], n) + gather_y(terms[9:], n)
            ys, qb = lax.optimization_barrier((ys, q4))
    grad_k = unroute(terms[:9], ys[0], ys[1], n, half, core)
    grad_v = unroute(terms[9:], ys[2], ys[3], n, half, core)

    dq = (acc * SCALE).astype(jnp.bfloat16).reshape(heads_kv, width, groups, tok)
    grad_query = dq.transpose(3, 0, 2, 1).reshape(tok, heads_q, width)
    return (grad_query, grad_k[0].transpose(1, 0, 2), grad_v[0].transpose(1, 0, 2))


def solution(mesh):
    placed = (
        P(("dp", "seq"), None, None),
        P(("dp", "seq"), None, None),
        P(("dp", "seq"), None, None),
        P(("dp", "seq"), None, None),
        P(("dp", "seq"), None, None),
        P(None, ("dp", "seq")),
    )
    return jax.shard_map(
        per_device,
        mesh=mesh,
        in_specs=placed,
        out_specs=(
            P(("dp", "seq"), None, None),
            P(("dp", "seq"), None, None),
            P(("dp", "seq"), None, None),
        ),
        check_vma=False,
    )
```

```python
import functools

import jax
import jax.numpy as jnp
from jax import lax
from jax.experimental import pallas as pl
from jax.experimental.pallas import tpu as pltpu
from jax.sharding import PartitionSpec as P

WINDOW = 1024
HOPS = 8
PLANE = 4
HEADS_PER_STEP = 2

SCALE = 168.0 ** (-0.5)


def shift(x, n, distance):
    pairs = [(i, i + distance) for i in range(n) if 0 <= i + distance < n]
    return lax.ppermute(x, "seq", pairs)


def swap(x, n, bit):
    return lax.ppermute(x, "seq", [(i, i ^ bit) for i in range(n)])


def one_way(x, n, bit, side):
    pairs = [(i, i ^ bit) for i in range(n) if (i & bit) == side]
    return lax.ppermute(x, "seq", pairs)


def _blocks_kernel(modes, has_acc, valid_ref, q_ref, do_ref, lse_ref, delta_ref, *refs):
    nb = len(modes)
    if has_acc:
        acc_ref = refs[0]
        refs = refs[1:]
    k_refs = refs[:nb]
    v_refs = refs[nb:2 * nb]
    dq_ref = refs[2 * nb]
    dk_refs = refs[2 * nb + 1:3 * nb + 1]
    dv_refs = refs[3 * nb + 1:]
    gb, grp, tok, width = q_ref.shape
    rows = grp * tok
    kk = lax.broadcasted_iota(jnp.int32, (tok, rows), 0)
    tt = lax.broadcasted_iota(jnp.int32, (tok, rows), 1) % tok
    causal = kk <= tt
    strict = kk > tt
    for g in range(gb):
        q = q_ref[g].reshape(rows, width)
        do = do_ref[g].reshape(rows, width)
        lse = lse_ref[g]
        delta = delta_ref[g]
        if has_acc:
            dq = acc_ref[g]
        else:
            dq = jnp.zeros((width, rows), jnp.float32)
        for b, mode in enumerate(modes):
            k = k_refs[b][0, g]
            v = v_refs[b][0, g]
            off = jnp.where(valid_ref[b] > 0, 0.0, 1e30).astype(jnp.float32)
            s = lax.dot_general(k, q, (((1,), (1,)), ((), ())), preferred_element_type=jnp.float32)
            e = jnp.exp(s * SCALE - lse - off)
            if mode == 0:
                p = jnp.where(causal, e, 0.0)
            elif mode == 2:
                p = jnp.where(strict, e, 0.0)
            else:
                p = e
            dp = lax.dot_general(v, do, (((1,), (1,)), ((), ())), preferred_element_type=jnp.float32)
            ds = p * (dp - delta)
            pb = p.astype(jnp.bfloat16)
            dsb = ds.astype(jnp.bfloat16)
            dv = jnp.dot(pb, do, preferred_element_type=jnp.float32)
            dk = jnp.dot(dsb, q, preferred_element_type=jnp.float32) * SCALE
            dq = dq + lax.dot_general(k, dsb, (((0,), (0,)), ((), ())), preferred_element_type=jnp.float32)
            dk_refs[b][0, g] = dk.astype(jnp.bfloat16)
            dv_refs[b][0, g] = dv.astype(jnp.bfloat16)
        dq_ref[g] = dq


def attend_blocks(modes, dist, idx, q4, do4, lse3, delta3, acc, kvs):
    nh, grp, tok, width = q4.shape
    gb = HEADS_PER_STEP
    nb = len(modes)
    valid = jnp.stack([(idx >= d).astype(jnp.int32) for d in dist])
    hspec = pl.BlockSpec((gb, grp, tok, width), lambda i, v: (i, 0, 0, 0))
    tspec = pl.BlockSpec((gb, width, grp * tok), lambda i, v: (i, 0, 0))
    rspec = pl.BlockSpec((gb, 1, grp * tok), lambda i, v: (i, 0, 0))
    kvspec = pl.BlockSpec((1, gb, tok, width), lambda i, v: (0, i, 0, 0))
    accs = [] if acc is None else [acc]
    out_shape = [jax.ShapeDtypeStruct((nh, width, grp * tok), jnp.float32)]
    out_shape += [jax.ShapeDtypeStruct(kv.shape, jnp.bfloat16) for kv in kvs]
    grid_spec = pltpu.PrefetchScalarGridSpec(
        num_scalar_prefetch=1,
        grid=(nh // gb,),
        in_specs=[hspec, hspec, rspec, rspec] + [tspec] * len(accs) + [kvspec] * (2 * nb),
        out_specs=[tspec] + [kvspec] * (2 * nb),
    )
    scores = nh * grp * tok * tok * nb
    cost = pl.CostEstimate(
        flops=10 * scores * width,
        transcendentals=scores,
        bytes_accessed=(2 + 2 * len(accs)) * q4.size * 2 + 2 * sum(kv.size for kv in kvs) * 2,
    )
    outs = pl.pallas_call(
        functools.partial(_blocks_kernel, tuple(modes), acc is not None),
        grid_spec=grid_spec,
        out_shape=out_shape,
        cost_estimate=cost,
        compiler_params=pltpu.CompilerParams(dimension_semantics=("arbitrary",)),
    )(valid, q4, do4, lse3, delta3, *accs, *kvs)
    return outs[0], list(outs[1:])


def route(x0, n, half, core):
    x1 = shift(x0, n, PLANE)
    ya = one_way(x0, n, 2, 0)
    cx1 = swap(x1, n, 1)
    yb = one_way(x1, n, 2, 2)
    x2 = shift(x1, n, PLANE)
    ca = one_way(x0, n, 1, 0)
    cb = one_way(x2, n, 1, 1)
    yc = one_way(x1, n, 2, 0)
    yd = one_way(x2, n, 2, 2)
    y0 = jnp.where(half == 1, ya, yb)
    cxo = jnp.where(core == 1, ca, cb)
    y1 = jnp.where(half == 1, yc, yd)
    return [x0, x1, cx1, x2, cxo, y0, None, y1, None]


def gather_y(terms, n):
    tx0, tx1, tcx1, tx2, tcxo, ty0, td0, ty1, td1 = terms
    f32 = jnp.float32
    bf16 = jnp.bfloat16
    ys0 = (ty0.astype(f32) + swap(td0, n, 1).astype(f32)).astype(bf16)
    ys1 = (ty1.astype(f32) + swap(td1, n, 1).astype(f32)).astype(bf16)
    return ys0, ys1


def unroute(terms, ys0, ys1, n, half, core):
    tx0, tx1, tcx1, tx2, tcxo, ty0, td0, ty1, td1 = terms
    f32 = jnp.float32
    bf16 = jnp.bfloat16
    yret0 = swap(ys0, n, 2).astype(f32)
    yret1 = swap(ys1, n, 2).astype(f32)
    ro = swap(tcxo, n, 1).astype(f32)
    r1 = swap(tcx1, n, 1).astype(f32)
    zero = jnp.zeros_like(r1)
    lo = half == 0
    part2 = tx2.astype(f32) + jnp.where(core == 1, ro, zero) + jnp.where(lo, zero, yret1)
    part1 = tx1.astype(f32) + r1 + jnp.where(lo, yret1, yret0)
    part1 = part1 + shift(part2.astype(bf16), n, -PLANE).astype(f32)
    part0 = tx0.astype(f32) + jnp.where(core == 0, ro, zero) + jnp.where(lo, yret0, zero)
    part0 = part0 + shift(part1.astype(bf16), n, -PLANE).astype(f32)
    return part0.astype(bf16)


def per_device(query, normed_key_rows, value_rows, out_in, grad_out, lse):
    tok, heads_q, width = query.shape
    heads_kv = normed_key_rows.shape[1]
    groups = heads_q // heads_kv
    n = lax.axis_size("seq")
    assert HOPS == 2 * PLANE
    idx = lax.axis_index("seq")
    half = (idx % PLANE) // 2
    core = idx % 2

    q4 = query.transpose(1, 0, 2).reshape(heads_kv, groups, tok, width)
    do4 = grad_out.transpose(1, 0, 2).reshape(heads_kv, groups, tok, width)
    delta = jnp.sum(grad_out.astype(jnp.float32) * out_in.astype(jnp.float32), axis=-1)
    delta3 = delta.T.reshape(heads_kv, 1, groups * tok)
    lse3 = lse.reshape(heads_kv, 1, groups * tok)
    kb = route(normed_key_rows.transpose(1, 0, 2)[None], n, half, core)
    vb = route(value_rows.transpose(1, 0, 2)[None], n, half, core)

    modes = [0, 1, 1, 2, 1, 1, 1, 1, 1]
    dist = [0, PLANE, 3 + 2 * core, 2 * PLANE, 7 - 6 * core, 2, 1 + 2 * core, 6, 5 + 2 * core]
    terms = [None] * 18

    def run(sel, acc, q):
        acc, out = attend_blocks(
            [modes[j] for j in sel], [dist[j] for j in sel], idx, q, do4, lse3, delta3, acc,
            [kb[j] for j in sel] + [vb[j] for j in sel])
        for m, j in enumerate(sel):
            terms[j] = out[m]
            terms[9 + j] = out[len(sel) + m]
        return acc

    acc = run([0, 1, 2], None, q4)
    (kb[5], vb[5]), acc = lax.optimization_barrier(((kb[5], vb[5]), acc))
    kb[6], vb[6] = swap(kb[5], n, 1), swap(vb[5], n, 1)
    kb[8], vb[8] = swap(kb[7], n, 1), swap(vb[7], n, 1)
    acc = run([3, 4, 5, 6, 7, 8], acc, q4)
    ys = gather_y(terms[:9], n) + gather_y(terms[9:], n)
    grad_k = unroute(terms[:9], ys[0], ys[1], n, half, core)
    grad_v = unroute(terms[9:], ys[2], ys[3], n, half, core)

    dq = (acc * SCALE).astype(jnp.bfloat16).reshape(heads_kv, width, groups, tok)
    grad_query = dq.transpose(3, 0, 2, 1).reshape(tok, heads_q, width)
    return (grad_query, grad_k[0].transpose(1, 0, 2), grad_v[0].transpose(1, 0, 2))


def solution(mesh):
    placed = (
        P(("dp", "seq"), None, None),
        P(("dp", "seq"), None, None),
        P(("dp", "seq"), None, None),
        P(("dp", "seq"), None, None),
        P(("dp", "seq"), None, None),
        P(None, ("dp", "seq")),
    )
    return jax.shard_map(
        per_device,
        mesh=mesh,
        in_specs=placed,
        out_specs=(
            P(("dp", "seq"), None, None),
            P(("dp", "seq"), None, None),
            P(("dp", "seq"), None, None),
        ),
        check_vma=False,
    )
```

```python
import functools

import jax
import jax.numpy as jnp
from jax import lax
from jax.experimental import pallas as pl
from jax.experimental.pallas import tpu as pltpu
from jax.sharding import PartitionSpec as P

WINDOW = 1024
HOPS = 8
PLANE = 4
HEADS_PER_STEP = 2

SCALE = 168.0 ** (-0.5)


def shift(x, n, distance):
    pairs = [(i, i + distance) for i in range(n) if 0 <= i + distance < n]
    return lax.ppermute(x, "seq", pairs)


def swap(x, n, bit):
    return lax.ppermute(x, "seq", [(i, i ^ bit) for i in range(n)])


def one_way(x, n, bit, side):
    pairs = [(i, i ^ bit) for i in range(n) if (i & bit) == side]
    return lax.ppermute(x, "seq", pairs)


def _blocks_kernel(modes, has_acc, valid_ref, q_ref, do_ref, lse_ref, delta_ref, *refs):
    nb = len(modes)
    if has_acc:
        acc_ref = refs[0]
        refs = refs[1:]
    k_refs = refs[:nb]
    v_refs = refs[nb:2 * nb]
    dq_ref = refs[2 * nb]
    dk_refs = refs[2 * nb + 1:3 * nb + 1]
    dv_refs = refs[3 * nb + 1:]
    gb, grp, tok, width = q_ref.shape
    rows = grp * tok
    kk = lax.broadcasted_iota(jnp.int32, (tok, rows), 0)
    tt = lax.broadcasted_iota(jnp.int32, (tok, rows), 1) % tok
    causal = kk <= tt
    strict = kk > tt
    for g in range(gb):
        q = q_ref[g].reshape(rows, width)
        do = do_ref[g].reshape(rows, width)
        lse = lse_ref[g]
        delta = delta_ref[g]
        if has_acc:
            dq = acc_ref[g]
        else:
            dq = jnp.zeros((width, rows), jnp.float32)
        for b, mode in enumerate(modes):
            k = k_refs[b][0, g]
            v = v_refs[b][0, g]
            off = jnp.where(valid_ref[b] > 0, 0.0, 1e30).astype(jnp.float32)
            s = lax.dot_general(k, q, (((1,), (1,)), ((), ())), preferred_element_type=jnp.float32)
            e = jnp.exp(s * SCALE - lse - off)
            if mode == 0:
                p = jnp.where(causal, e, 0.0)
            elif mode == 2:
                p = jnp.where(strict, e, 0.0)
            else:
                p = e
            dp = lax.dot_general(v, do, (((1,), (1,)), ((), ())), preferred_element_type=jnp.float32)
            ds = p * (dp - delta)
            pb = p.astype(jnp.bfloat16)
            dsb = ds.astype(jnp.bfloat16)
            dv = jnp.dot(pb, do, preferred_element_type=jnp.float32)
            dk = jnp.dot(dsb, q, preferred_element_type=jnp.float32) * SCALE
            dq = dq + lax.dot_general(k, dsb, (((0,), (0,)), ((), ())), preferred_element_type=jnp.float32)
            dk_refs[b][0, g] = dk.astype(jnp.bfloat16)
            dv_refs[b][0, g] = dv.astype(jnp.bfloat16)
        dq_ref[g] = dq


def attend_blocks(modes, dist, idx, q4, do4, lse3, delta3, acc, kvs, heads=None):
    nh, grp, tok, width = q4.shape
    gb = HEADS_PER_STEP
    h0, h1 = (0, nh) if heads is None else heads
    o = h0 // gb
    nb = len(modes)
    valid = jnp.stack([(idx >= d).astype(jnp.int32) for d in dist])
    nsel = h1 - h0
    hspec = pl.BlockSpec((gb, grp, tok, width), lambda i, v: (i + o, 0, 0, 0))
    tspec = pl.BlockSpec((gb, width, grp * tok), lambda i, v: (i, 0, 0))
    rspec = pl.BlockSpec((gb, 1, grp * tok), lambda i, v: (i + o, 0, 0))
    kvspec = pl.BlockSpec((1, gb, tok, width), lambda i, v: (0, i + o, 0, 0))
    outspec = pl.BlockSpec((1, gb, tok, width), lambda i, v: (0, i, 0, 0))
    accs = [] if acc is None else [acc]
    out_shape = [jax.ShapeDtypeStruct((nsel, width, grp * tok), jnp.float32)]
    out_shape += [jax.ShapeDtypeStruct((1, nsel) + kv.shape[2:], jnp.bfloat16) for kv in kvs]
    grid_spec = pltpu.PrefetchScalarGridSpec(
        num_scalar_prefetch=1,
        grid=(nsel // gb,),
        in_specs=[hspec, hspec, rspec, rspec] + [tspec] * len(accs) + [kvspec] * (2 * nb),
        out_specs=[tspec] + [outspec] * (2 * nb),
    )
    scores = nsel * grp * tok * tok * nb
    cost = pl.CostEstimate(
        flops=10 * scores * width,
        transcendentals=scores,
        bytes_accessed=((2 + 2 * len(accs)) * q4.size * 2 + 2 * sum(kv.size for kv in kvs) * 2) * nsel // nh,
    )
    outs = pl.pallas_call(
        functools.partial(_blocks_kernel, tuple(modes), acc is not None),
        grid_spec=grid_spec,
        out_shape=out_shape,
        cost_estimate=cost,
        compiler_params=pltpu.CompilerParams(dimension_semantics=("arbitrary",)),
    )(valid, q4, do4, lse3, delta3, *accs, *kvs)
    return outs[0], list(outs[1:])


def route(x0, n, half, core):
    x1 = shift(x0, n, PLANE)
    ya = one_way(x0, n, 2, 0)
    cx1 = swap(x1, n, 1)
    yb = one_way(x1, n, 2, 2)
    x2 = shift(x1, n, PLANE)
    ca = one_way(x0, n, 1, 0)
    cb = one_way(x2, n, 1, 1)
    yc = one_way(x1, n, 2, 0)
    yd = one_way(x2, n, 2, 2)
    y0 = jnp.where(half == 1, ya, yb)
    d0 = swap(y0, n, 1)
    cxo = jnp.where(core == 1, ca, cb)
    y1 = jnp.where(half == 1, yc, yd)
    d1 = swap(y1, n, 1)
    return [x0, x1, cx1, x2, cxo, y0, d0, y1, d1]


def gather_y(terms, n):
    tx0, tx1, tcx1, tx2, tcxo, ty0, td0, ty1, td1 = terms
    f32 = jnp.float32
    bf16 = jnp.bfloat16
    ys0 = (ty0.astype(f32) + swap(td0, n, 1).astype(f32)).astype(bf16)
    ys1 = (ty1.astype(f32) + swap(td1, n, 1).astype(f32)).astype(bf16)
    return ys0, ys1


def unroute(terms, ys0, ys1, n, half, core):
    tx0, tx1, tcx1, tx2, tcxo, ty0, td0, ty1, td1 = terms
    f32 = jnp.float32
    bf16 = jnp.bfloat16
    yret0 = swap(ys0, n, 2).astype(f32)
    yret1 = swap(ys1, n, 2).astype(f32)
    ro = swap(tcxo, n, 1).astype(f32)
    r1 = swap(tcx1, n, 1).astype(f32)
    zero = jnp.zeros_like(r1)
    lo = half == 0
    part2 = tx2.astype(f32) + jnp.where(core == 1, ro, zero) + jnp.where(lo, zero, yret1)
    part1 = tx1.astype(f32) + r1 + jnp.where(lo, yret1, yret0)
    part1 = part1 + shift(part2.astype(bf16), n, -PLANE).astype(f32)
    part0 = tx0.astype(f32) + jnp.where(core == 0, ro, zero) + jnp.where(lo, yret0, zero)
    part0 = part0 + shift(part1.astype(bf16), n, -PLANE).astype(f32)
    return part0.astype(bf16)


def per_device(query, normed_key_rows, value_rows, out_in, grad_out, lse):
    tok, heads_q, width = query.shape
    heads_kv = normed_key_rows.shape[1]
    groups = heads_q // heads_kv
    n = lax.axis_size("seq")
    assert HOPS == 2 * PLANE
    idx = lax.axis_index("seq")
    half = (idx % PLANE) // 2
    core = idx % 2

    q4 = query.transpose(1, 0, 2).reshape(heads_kv, groups, tok, width)
    do4 = grad_out.transpose(1, 0, 2).reshape(heads_kv, groups, tok, width)
    delta = jnp.sum(grad_out.astype(jnp.float32) * out_in.astype(jnp.float32), axis=-1)
    delta3 = delta.T.reshape(heads_kv, 1, groups * tok)
    lse3 = lse.reshape(heads_kv, 1, groups * tok)
    kb = route(normed_key_rows.transpose(1, 0, 2)[None], n, half, core)
    vb = route(value_rows.transpose(1, 0, 2)[None], n, half, core)

    late = [3, 4, 5, 6, 7, 8]
    early = [0, 1, 2]
    modes = [0, 1, 1, 2, 1, 1, 1, 1, 1]
    dist = [0, PLANE, 3 + 2 * core, 2 * PLANE, 7 - 6 * core, 2, 1 + 2 * core, 6, 5 + 2 * core]
    spans = ((0, heads_kv // 2), (heads_kv // 2, heads_kv))
    qb = q4
    accs = []
    halves = []
    for span in spans:
        acc, out = attend_blocks(
            [modes[j] for j in late], [dist[j] for j in late], idx, qb, do4, lse3, delta3, None,
            [kb[j] for j in late] + [vb[j] for j in late], heads=span)
        accs.append(acc)
        tk = [None] * 9
        tv = [None] * 9
        for m, j in enumerate(late):
            tk[j] = out[m]
            tv[j] = out[len(late) + m]
        ys = gather_y(tk, n) + gather_y(tv, n)
        ys, qb = lax.optimization_barrier((ys, q4))
        halves.append((tk, tv, ys))
    acc, out = attend_blocks(
        [modes[j] for j in early], [dist[j] for j in early], idx, qb, do4, lse3, delta3,
        jnp.concatenate(accs, axis=0), [kb[j] for j in early] + [vb[j] for j in early])
    gk = []
    gv = []
    for (h0, h1), (tk, tv, ys) in zip(spans, halves):
        for m, j in enumerate(early):
            tk[j] = out[m][:, h0:h1]
            tv[j] = out[len(early) + m][:, h0:h1]
        gk.append(unroute(tk, ys[0], ys[1], n, half, core))
        gv.append(unroute(tv, ys[2], ys[3], n, half, core))
    grad_k = jnp.concatenate(gk, axis=1)
    grad_v = jnp.concatenate(gv, axis=1)

    dq = (acc * SCALE).astype(jnp.bfloat16).reshape(heads_kv, width, groups, tok)
    grad_query = dq.transpose(3, 0, 2, 1).reshape(tok, heads_q, width)
    return (grad_query, grad_k[0].transpose(1, 0, 2), grad_v[0].transpose(1, 0, 2))


def solution(mesh):
    placed = (
        P(("dp", "seq"), None, None),
        P(("dp", "seq"), None, None),
        P(("dp", "seq"), None, None),
        P(("dp", "seq"), None, None),
        P(("dp", "seq"), None, None),
        P(None, ("dp", "seq")),
    )
    return jax.shard_map(
        per_device,
        mesh=mesh,
        in_specs=placed,
        out_specs=(
            P(("dp", "seq"), None, None),
            P(("dp", "seq"), None, None),
            P(("dp", "seq"), None, None),
        ),
        check_vma=False,
    )
```

```python
import functools

import jax
import jax.numpy as jnp
from jax import lax
from jax.experimental import pallas as pl
from jax.experimental.pallas import tpu as pltpu
from jax.sharding import PartitionSpec as P

WINDOW = 1024
HOPS = 8
PLANE = 4
HEADS_PER_STEP = 4

SCALE = 168.0 ** (-0.5)


def shift(x, n, distance):
    pairs = [(i, i + distance) for i in range(n) if 0 <= i + distance < n]
    return lax.ppermute(x, "seq", pairs)


def swap(x, n, bit):
    return lax.ppermute(x, "seq", [(i, i ^ bit) for i in range(n)])


def one_way(x, n, bit, side):
    pairs = [(i, i ^ bit) for i in range(n) if (i & bit) == side]
    return lax.ppermute(x, "seq", pairs)


def _blocks_kernel(modes, has_acc, valid_ref, q_ref, do_ref, lse_ref, delta_ref, *refs):
    nb = len(modes)
    if has_acc:
        acc_ref = refs[0]
        refs = refs[1:]
    k_refs = refs[:nb]
    v_refs = refs[nb:2 * nb]
    dq_ref = refs[2 * nb]
    dk_refs = refs[2 * nb + 1:3 * nb + 1]
    dv_refs = refs[3 * nb + 1:]
    gb, grp, tok, width = q_ref.shape
    rows = grp * tok
    kk = lax.broadcasted_iota(jnp.int32, (tok, rows), 0)
    tt = lax.broadcasted_iota(jnp.int32, (tok, rows), 1) % tok
    causal = kk <= tt
    strict = kk > tt
    for g in range(gb):
        q = q_ref[g].reshape(rows, width)
        do = do_ref[g].reshape(rows, width)
        lse = lse_ref[g]
        delta = delta_ref[g]
        if has_acc:
            dq = acc_ref[g]
        else:
            dq = jnp.zeros((width, rows), jnp.float32)
        for b, mode in enumerate(modes):
            k = k_refs[b][0, g]
            v = v_refs[b][0, g]
            off = jnp.where(valid_ref[b] > 0, 0.0, 1e30).astype(jnp.float32)
            s = lax.dot_general(k, q, (((1,), (1,)), ((), ())), preferred_element_type=jnp.float32)
            e = jnp.exp(s * SCALE - lse - off)
            if mode == 0:
                p = jnp.where(causal, e, 0.0)
            elif mode == 2:
                p = jnp.where(strict, e, 0.0)
            else:
                p = e
            dp = lax.dot_general(v, do, (((1,), (1,)), ((), ())), preferred_element_type=jnp.float32)
            ds = p * (dp - delta)
            pb = p.astype(jnp.bfloat16)
            dsb = ds.astype(jnp.bfloat16)
            dv = jnp.dot(pb, do, preferred_element_type=jnp.float32)
            dk = jnp.dot(dsb, q, preferred_element_type=jnp.float32) * SCALE
            dq = dq + lax.dot_general(k, dsb, (((0,), (0,)), ((), ())), preferred_element_type=jnp.float32)
            dk_refs[b][0, g] = dk.astype(jnp.bfloat16)
            dv_refs[b][0, g] = dv.astype(jnp.bfloat16)
        dq_ref[g] = dq


def attend_blocks(modes, dist, idx, q4, do4, lse3, delta3, acc, kvs):
    nh, grp, tok, width = q4.shape
    gb = HEADS_PER_STEP
    nb = len(modes)
    valid = jnp.stack([(idx >= d).astype(jnp.int32) for d in dist])
    hspec = pl.BlockSpec((gb, grp, tok, width), lambda i, v: (i, 0, 0, 0))
    tspec = pl.BlockSpec((gb, width, grp * tok), lambda i, v: (i, 0, 0))
    rspec = pl.BlockSpec((gb, 1, grp * tok), lambda i, v: (i, 0, 0))
    kvspec = pl.BlockSpec((1, gb, tok, width), lambda i, v: (0, i, 0, 0))
    accs = [] if acc is None else [acc]
    out_shape = [jax.ShapeDtypeStruct((nh, width, grp * tok), jnp.float32)]
    out_shape += [jax.ShapeDtypeStruct(kv.shape, jnp.bfloat16) for kv in kvs]
    grid_spec = pltpu.PrefetchScalarGridSpec(
        num_scalar_prefetch=1,
        grid=(nh // gb,),
        in_specs=[hspec, hspec, rspec, rspec] + [tspec] * len(accs) + [kvspec] * (2 * nb),
        out_specs=[tspec] + [kvspec] * (2 * nb),
    )
    scores = nh * grp * tok * tok * nb
    cost = pl.CostEstimate(
        flops=10 * scores * width,
        transcendentals=scores,
        bytes_accessed=(2 + 2 * len(accs)) * q4.size * 2 + 2 * sum(kv.size for kv in kvs) * 2,
    )
    outs = pl.pallas_call(
        functools.partial(_blocks_kernel, tuple(modes), acc is not None),
        grid_spec=grid_spec,
        out_shape=out_shape,
        cost_estimate=cost,
        compiler_params=pltpu.CompilerParams(dimension_semantics=("arbitrary",)),
    )(valid, q4, do4, lse3, delta3, *accs, *kvs)
    return outs[0], list(outs[1:])


def route(x0, n, half, core):
    x1 = shift(x0, n, PLANE)
    ya = one_way(x0, n, 2, 0)
    cx1 = swap(x1, n, 1)
    yb = one_way(x1, n, 2, 2)
    x2 = shift(x1, n, PLANE)
    ca = one_way(x0, n, 1, 0)
    cb = one_way(x2, n, 1, 1)
    yc = one_way(x1, n, 2, 0)
    yd = one_way(x2, n, 2, 2)
    y0 = jnp.where(half == 1, ya, yb)
    d0 = swap(y0, n, 1)
    cxo = jnp.where(core == 1, ca, cb)
    y1 = jnp.where(half == 1, yc, yd)
    d1 = swap(y1, n, 1)
    return [x0, x1, cx1, x2, cxo, y0, d0, y1, d1]


def gather_y(terms, n):
    tx0, tx1, tcx1, tx2, tcxo, ty0, td0, ty1, td1 = terms
    f32 = jnp.float32
    bf16 = jnp.bfloat16
    ys0 = (ty0.astype(f32) + swap(td0, n, 1).astype(f32)).astype(bf16)
    ys1 = (ty1.astype(f32) + swap(td1, n, 1).astype(f32)).astype(bf16)
    return ys0, ys1


def unroute(terms, ys0, ys1, n, half, core):
    tx0, tx1, tcx1, tx2, tcxo, ty0, td0, ty1, td1 = terms
    f32 = jnp.float32
    bf16 = jnp.bfloat16
    yret0 = swap(ys0, n, 2).astype(f32)
    yret1 = swap(ys1, n, 2).astype(f32)
    ro = swap(tcxo, n, 1).astype(f32)
    r1 = swap(tcx1, n, 1).astype(f32)
    zero = jnp.zeros_like(r1)
    lo = half == 0
    part2 = tx2.astype(f32) + jnp.where(core == 1, ro, zero) + jnp.where(lo, zero, yret1)
    part1 = tx1.astype(f32) + r1 + jnp.where(lo, yret1, yret0)
    part1 = part1 + shift(part2.astype(bf16), n, -PLANE).astype(f32)
    part0 = tx0.astype(f32) + jnp.where(core == 0, ro, zero) + jnp.where(lo, yret0, zero)
    part0 = part0 + shift(part1.astype(bf16), n, -PLANE).astype(f32)
    return part0.astype(bf16)


def per_device(query, normed_key_rows, value_rows, out_in, grad_out, lse):
    tok, heads_q, width = query.shape
    heads_kv = normed_key_rows.shape[1]
    groups = heads_q // heads_kv
    n = lax.axis_size("seq")
    assert HOPS == 2 * PLANE
    idx = lax.axis_index("seq")
    half = (idx % PLANE) // 2
    core = idx % 2

    q4 = query.transpose(1, 0, 2).reshape(heads_kv, groups, tok, width)
    do4 = grad_out.transpose(1, 0, 2).reshape(heads_kv, groups, tok, width)
    delta = jnp.sum(grad_out.astype(jnp.float32) * out_in.astype(jnp.float32), axis=-1)
    delta3 = delta.T.reshape(heads_kv, 1, groups * tok)
    lse3 = lse.reshape(heads_kv, 1, groups * tok)
    kb = route(normed_key_rows.transpose(1, 0, 2)[None], n, half, core)
    vb = route(value_rows.transpose(1, 0, 2)[None], n, half, core)

    late = [3, 4, 5, 6, 7, 8]
    early = [0, 1, 2]
    modes = [0, 1, 1, 2, 1, 1, 1, 1, 1]
    dist = [0, PLANE, 3 + 2 * core, 2 * PLANE, 7 - 6 * core, 2, 1 + 2 * core, 6, 5 + 2 * core]
    terms = [None] * 18
    acc = None
    ys = None
    qb = q4
    for sel in (late, early):
        acc, out = attend_blocks(
            [modes[j] for j in sel], [dist[j] for j in sel], idx, qb, do4, lse3, delta3, acc,
            [kb[j] for j in sel] + [vb[j] for j in sel])
        for m, j in enumerate(sel):
            terms[j] = out[m]
            terms[9 + j] = out[len(sel) + m]
        if ys is None:
            ys = gather_y(terms[:9], n) + gather_y(terms[9:], n)
            ys, qb = lax.optimization_barrier((ys, q4))
    grad_k = unroute(terms[:9], ys[0], ys[1], n, half, core)
    grad_v = unroute(terms[9:], ys[2], ys[3], n, half, core)

    dq = (acc * SCALE).astype(jnp.bfloat16).reshape(heads_kv, width, groups, tok)
    grad_query = dq.transpose(3, 0, 2, 1).reshape(tok, heads_q, width)
    return (grad_query, grad_k[0].transpose(1, 0, 2), grad_v[0].transpose(1, 0, 2))


def solution(mesh):
    placed = (
        P(("dp", "seq"), None, None),
        P(("dp", "seq"), None, None),
        P(("dp", "seq"), None, None),
        P(("dp", "seq"), None, None),
        P(("dp", "seq"), None, None),
        P(None, ("dp", "seq")),
    )
    return jax.shard_map(
        per_device,
        mesh=mesh,
        in_specs=placed,
        out_specs=(
            P(("dp", "seq"), None, None),
            P(("dp", "seq"), None, None),
            P(("dp", "seq"), None, None),
        ),
        check_vma=False,
    )
```

```python
import functools

import jax
import jax.numpy as jnp
from jax import lax
from jax.experimental import pallas as pl
from jax.experimental.pallas import tpu as pltpu
from jax.sharding import PartitionSpec as P

WINDOW = 1024
HOPS = 8
PLANE = 4
HEADS_PER_STEP = 4

SCALE = 168.0 ** (-0.5)


def shift(x, n, distance):
    pairs = [(i, i + distance) for i in range(n) if 0 <= i + distance < n]
    return lax.ppermute(x, "seq", pairs)


def swap(x, n, bit):
    return lax.ppermute(x, "seq", [(i, i ^ bit) for i in range(n)])


def one_way(x, n, bit, side):
    pairs = [(i, i ^ bit) for i in range(n) if (i & bit) == side]
    return lax.ppermute(x, "seq", pairs)


def _blocks_kernel(modes, has_acc, valid_ref, q_ref, do_ref, lse_ref, delta_ref, *refs):
    nb = len(modes)
    if has_acc:
        acc_ref = refs[0]
        refs = refs[1:]
    k_refs = refs[:nb]
    v_refs = refs[nb:2 * nb]
    dq_ref = refs[2 * nb]
    dk_refs = refs[2 * nb + 1:3 * nb + 1]
    dv_refs = refs[3 * nb + 1:]
    gb, grp, tok, width = q_ref.shape
    rows = grp * tok
    kk = lax.broadcasted_iota(jnp.int32, (tok, rows), 0)
    tt = lax.broadcasted_iota(jnp.int32, (tok, rows), 1) % tok
    causal = kk <= tt
    strict = kk > tt
    for g in range(gb):
        q = q_ref[g].reshape(rows, width)
        do = do_ref[g].reshape(rows, width)
        lse = lse_ref[g]
        delta = delta_ref[g]
        if has_acc:
            dq = acc_ref[g]
        else:
            dq = jnp.zeros((width, rows), jnp.float32)
        for b, mode in enumerate(modes):
            k = k_refs[b][0, g]
            v = v_refs[b][0, g]
            off = jnp.where(valid_ref[b] > 0, 0.0, 1e30).astype(jnp.float32)
            s = lax.dot_general(k, q, (((1,), (1,)), ((), ())), preferred_element_type=jnp.float32)
            e = jnp.exp(s * SCALE - lse - off)
            if mode == 0:
                p = jnp.where(causal, e, 0.0)
            elif mode == 2:
                p = jnp.where(strict, e, 0.0)
            else:
                p = e
            dp = lax.dot_general(v, do, (((1,), (1,)), ((), ())), preferred_element_type=jnp.float32)
            ds = p * (dp - delta)
            pb = p.astype(jnp.bfloat16)
            dsb = ds.astype(jnp.bfloat16)
            dv = jnp.dot(pb, do, preferred_element_type=jnp.float32)
            dk = jnp.dot(dsb, q, preferred_element_type=jnp.float32) * SCALE
            dq = dq + lax.dot_general(k, dsb, (((0,), (0,)), ((), ())), preferred_element_type=jnp.float32)
            dk_refs[b][0, g] = dk.astype(jnp.bfloat16)
            dv_refs[b][0, g] = dv.astype(jnp.bfloat16)
        dq_ref[g] = dq


def attend_blocks(modes, dist, idx, q4, do4, lse3, delta3, acc, kvs):
    nh, grp, tok, width = q4.shape
    gb = HEADS_PER_STEP
    nb = len(modes)
    valid = jnp.stack([(idx >= d).astype(jnp.int32) for d in dist])
    hspec = pl.BlockSpec((gb, grp, tok, width), lambda i, v: (i, 0, 0, 0))
    tspec = pl.BlockSpec((gb, width, grp * tok), lambda i, v: (i, 0, 0))
    rspec = pl.BlockSpec((gb, 1, grp * tok), lambda i, v: (i, 0, 0))
    kvspec = pl.BlockSpec((1, gb, tok, width), lambda i, v: (0, i, 0, 0))
    accs = [] if acc is None else [acc]
    out_shape = [jax.ShapeDtypeStruct((nh, width, grp * tok), jnp.float32)]
    out_shape += [jax.ShapeDtypeStruct(kv.shape, jnp.bfloat16) for kv in kvs]
    grid_spec = pltpu.PrefetchScalarGridSpec(
        num_scalar_prefetch=1,
        grid=(nh // gb,),
        in_specs=[hspec, hspec, rspec, rspec] + [tspec] * len(accs) + [kvspec] * (2 * nb),
        out_specs=[tspec] + [kvspec] * (2 * nb),
    )
    scores = nh * grp * tok * tok * nb
    cost = pl.CostEstimate(
        flops=10 * scores * width,
        transcendentals=scores,
        bytes_accessed=(2 + 2 * len(accs)) * q4.size * 2 + 2 * sum(kv.size for kv in kvs) * 2,
    )
    outs = pl.pallas_call(
        functools.partial(_blocks_kernel, tuple(modes), acc is not None),
        grid_spec=grid_spec,
        out_shape=out_shape,
        cost_estimate=cost,
        compiler_params=pltpu.CompilerParams(dimension_semantics=("arbitrary",)),
    )(valid, q4, do4, lse3, delta3, *accs, *kvs)
    return outs[0], list(outs[1:])


def route(x0, n, half, core):
    x1 = shift(x0, n, PLANE)
    ya = one_way(x0, n, 2, 0)
    cx1 = swap(x1, n, 1)
    yb = one_way(x1, n, 2, 2)
    x2 = shift(x1, n, PLANE)
    ca = one_way(x0, n, 1, 0)
    cb = one_way(x2, n, 1, 1)
    yc = one_way(x1, n, 2, 0)
    yd = one_way(x2, n, 2, 2)
    y0 = jnp.where(half == 1, ya, yb)
    d0 = swap(y0, n, 1)
    cxo = jnp.where(core == 1, ca, cb)
    y1 = jnp.where(half == 1, yc, yd)
    d1 = swap(y1, n, 1)
    return [x0, x1, cx1, x2, cxo, y0, d0, y1, d1]


def gather_y(terms, n):
    tx0, tx1, tcx1, tx2, tcxo, ty0, td0, ty1, td1 = terms
    f32 = jnp.float32
    bf16 = jnp.bfloat16
    ys0 = (ty0.astype(f32) + swap(td0, n, 1).astype(f32)).astype(bf16)
    ys1 = (ty1.astype(f32) + swap(td1, n, 1).astype(f32)).astype(bf16)
    return ys0, ys1


def unroute(terms, ys0, ys1, n, half, core):
    tx0, tx1, tcx1, tx2, tcxo, ty0, td0, ty1, td1 = terms
    f32 = jnp.float32
    bf16 = jnp.bfloat16
    yret0 = swap(ys0, n, 2).astype(f32)
    yret1 = swap(ys1, n, 2).astype(f32)
    ro = swap(tcxo, n, 1).astype(f32)
    r1 = swap(tcx1, n, 1).astype(f32)
    zero = jnp.zeros_like(r1)
    lo = half == 0
    part2 = tx2.astype(f32) + jnp.where(core == 1, ro, zero) + jnp.where(lo, zero, yret1)
    part1 = tx1.astype(f32) + r1 + jnp.where(lo, yret1, yret0)
    part1 = part1 + shift(part2.astype(bf16), n, -PLANE).astype(f32)
    part0 = tx0.astype(f32) + jnp.where(core == 0, ro, zero) + jnp.where(lo, yret0, zero)
    part0 = part0 + shift(part1.astype(bf16), n, -PLANE).astype(f32)
    return part0.astype(bf16)


def per_device(query, normed_key_rows, value_rows, out_in, grad_out, lse):
    tok, heads_q, width = query.shape
    heads_kv = normed_key_rows.shape[1]
    groups = heads_q // heads_kv
    n = lax.axis_size("seq")
    assert HOPS == 2 * PLANE
    idx = lax.axis_index("seq")
    half = (idx % PLANE) // 2
    core = idx % 2

    q4 = query.transpose(1, 0, 2).reshape(heads_kv, groups, tok, width)
    do4 = grad_out.transpose(1, 0, 2).reshape(heads_kv, groups, tok, width)
    delta = jnp.sum(grad_out.astype(jnp.float32) * out_in.astype(jnp.float32), axis=-1)
    delta3 = delta.T.reshape(heads_kv, 1, groups * tok)
    lse3 = lse.reshape(heads_kv, 1, groups * tok)
    kb = route(normed_key_rows.transpose(1, 0, 2)[None], n, half, core)
    vb = route(value_rows.transpose(1, 0, 2)[None], n, half, core)

    late = [5, 6, 7, 8]
    early = [0, 1, 2, 3, 4]
    modes = [0, 1, 1, 2, 1, 1, 1, 1, 1]
    dist = [0, PLANE, 3 + 2 * core, 2 * PLANE, 7 - 6 * core, 2, 1 + 2 * core, 6, 5 + 2 * core]
    terms = [None] * 18
    acc = None
    ys = None
    qb = q4
    for sel in (late, early):
        acc, out = attend_blocks(
            [modes[j] for j in sel], [dist[j] for j in sel], idx, qb, do4, lse3, delta3, acc,
            [kb[j] for j in sel] + [vb[j] for j in sel])
        for m, j in enumerate(sel):
            terms[j] = out[m]
            terms[9 + j] = out[len(sel) + m]
        if ys is None:
            ys = gather_y(terms[:9], n) + gather_y(terms[9:], n)
            ys, qb = lax.optimization_barrier((ys, q4))
    grad_k = unroute(terms[:9], ys[0], ys[1], n, half, core)
    grad_v = unroute(terms[9:], ys[2], ys[3], n, half, core)

    dq = (acc * SCALE).astype(jnp.bfloat16).reshape(heads_kv, width, groups, tok)
    grad_query = dq.transpose(3, 0, 2, 1).reshape(tok, heads_q, width)
    return (grad_query, grad_k[0].transpose(1, 0, 2), grad_v[0].transpose(1, 0, 2))


def solution(mesh):
    placed = (
        P(("dp", "seq"), None, None),
        P(("dp", "seq"), None, None),
        P(("dp", "seq"), None, None),
        P(("dp", "seq"), None, None),
        P(("dp", "seq"), None, None),
        P(None, ("dp", "seq")),
    )
    return jax.shard_map(
        per_device,
        mesh=mesh,
        in_specs=placed,
        out_specs=(
            P(("dp", "seq"), None, None),
            P(("dp", "seq"), None, None),
            P(("dp", "seq"), None, None),
        ),
        check_vma=False,
    )
```

```python
import functools

import jax
import jax.numpy as jnp
from jax import lax
from jax.experimental import pallas as pl
from jax.experimental.pallas import tpu as pltpu
from jax.sharding import PartitionSpec as P

WINDOW = 1024
HOPS = 8
PLANE = 4
HEADS_PER_STEP = 4

SCALE = 168.0 ** (-0.5)


def shift(x, n, distance):
    pairs = [(i, i + distance) for i in range(n) if 0 <= i + distance < n]
    return lax.ppermute(x, "seq", pairs)


def swap(x, n, bit):
    return lax.ppermute(x, "seq", [(i, i ^ bit) for i in range(n)])


def one_way(x, n, bit, side):
    pairs = [(i, i ^ bit) for i in range(n) if (i & bit) == side]
    return lax.ppermute(x, "seq", pairs)


def _blocks_kernel(modes, has_acc, valid_ref, q_ref, do_ref, lse_ref, delta_ref, *refs):
    nb = len(modes)
    if has_acc:
        acc_ref = refs[0]
        refs = refs[1:]
    k_refs = refs[:nb]
    v_refs = refs[nb:2 * nb]
    dq_ref = refs[2 * nb]
    dk_refs = refs[2 * nb + 1:3 * nb + 1]
    dv_refs = refs[3 * nb + 1:]
    gb, grp, tok, width = q_ref.shape
    rows = grp * tok
    kk = lax.broadcasted_iota(jnp.int32, (tok, rows), 0)
    tt = lax.broadcasted_iota(jnp.int32, (tok, rows), 1) % tok
    causal = kk <= tt
    strict = kk > tt
    for g in range(gb):
        q = q_ref[g].reshape(rows, width)
        do = do_ref[g].reshape(rows, width)
        lse = lse_ref[g]
        delta = delta_ref[g]
        if has_acc:
            dq = acc_ref[g]
        else:
            dq = jnp.zeros((width, rows), jnp.float32)
        for b, mode in enumerate(modes):
            k = k_refs[b][0, g]
            v = v_refs[b][0, g]
            off = jnp.where(valid_ref[b] > 0, 0.0, 1e30).astype(jnp.float32)
            s = lax.dot_general(k, q, (((1,), (1,)), ((), ())), preferred_element_type=jnp.float32)
            e = jnp.exp(s * SCALE - lse - off)
            if mode == 0:
                p = jnp.where(causal, e, 0.0)
            elif mode == 2:
                p = jnp.where(strict, e, 0.0)
            else:
                p = e
            dp = lax.dot_general(v, do, (((1,), (1,)), ((), ())), preferred_element_type=jnp.float32)
            ds = p * (dp - delta)
            pb = p.astype(jnp.bfloat16)
            dsb = ds.astype(jnp.bfloat16)
            dv = jnp.dot(pb, do, preferred_element_type=jnp.float32)
            dk = jnp.dot(dsb, q, preferred_element_type=jnp.float32) * SCALE
            dq = dq + lax.dot_general(k, dsb, (((0,), (0,)), ((), ())), preferred_element_type=jnp.float32)
            dk_refs[b][0, g] = dk.astype(jnp.bfloat16)
            dv_refs[b][0, g] = dv.astype(jnp.bfloat16)
        dq_ref[g] = dq


def attend_blocks(modes, dist, idx, q4, do4, lse3, delta3, acc, kvs):
    nh, grp, tok, width = q4.shape
    gb = HEADS_PER_STEP
    nb = len(modes)
    valid = jnp.stack([(idx >= d).astype(jnp.int32) for d in dist])
    hspec = pl.BlockSpec((gb, grp, tok, width), lambda i, v: (i, 0, 0, 0))
    tspec = pl.BlockSpec((gb, width, grp * tok), lambda i, v: (i, 0, 0))
    rspec = pl.BlockSpec((gb, 1, grp * tok), lambda i, v: (i, 0, 0))
    kvspec = pl.BlockSpec((1, gb, tok, width), lambda i, v: (0, i, 0, 0))
    kvspecs = [pl.BlockSpec((1, gb, tok, width), lambda i, v, s=s: (s, i, 0, 0)) for _, s in kvs]
    accs = [] if acc is None else [acc]
    out_shape = [jax.ShapeDtypeStruct((nh, width, grp * tok), jnp.float32)]
    out_shape += [jax.ShapeDtypeStruct((1,) + kv.shape[1:], jnp.bfloat16) for kv, _ in kvs]
    grid_spec = pltpu.PrefetchScalarGridSpec(
        num_scalar_prefetch=1,
        grid=(nh // gb,),
        in_specs=[hspec, hspec, rspec, rspec] + [tspec] * len(accs) + kvspecs,
        out_specs=[tspec] + [kvspec] * (2 * nb),
    )
    scores = nh * grp * tok * tok * nb
    cost = pl.CostEstimate(
        flops=10 * scores * width,
        transcendentals=scores,
        bytes_accessed=(2 + 2 * len(accs)) * q4.size * 2 + 2 * sum(kv.size // kv.shape[0] for kv, _ in kvs) * 2,
    )
    outs = pl.pallas_call(
        functools.partial(_blocks_kernel, tuple(modes), acc is not None),
        grid_spec=grid_spec,
        out_shape=out_shape,
        cost_estimate=cost,
        compiler_params=pltpu.CompilerParams(dimension_semantics=("arbitrary",)),
    )(valid, q4, do4, lse3, delta3, *accs, *[kv for kv, _ in kvs])
    return outs[0], list(outs[1:])


def route(k0, v0, n, half, core):
    def both(a, b):
        return jnp.concatenate([a, b], axis=0)

    x0 = (k0, v0)
    x1 = tuple(shift(x, n, PLANE) for x in x0)
    ya = tuple(one_way(x, n, 2, 0) for x in x0)
    cx1 = swap(both(*x1), n, 1)
    yb = tuple(one_way(x, n, 2, 2) for x in x1)
    x2 = tuple(shift(x, n, PLANE) for x in x1)
    ca = one_way(both(*x0), n, 1, 0)
    cb = one_way(both(*x2), n, 1, 1)
    yc = tuple(one_way(x, n, 2, 0) for x in x1)
    yd = tuple(one_way(x, n, 2, 2) for x in x2)
    y0 = tuple(jnp.where(half == 1, a, b) for a, b in zip(ya, yb))
    d0 = swap(both(*y0), n, 1)
    cxo = jnp.where(core == 1, ca, cb)
    y1 = tuple(jnp.where(half == 1, a, b) for a, b in zip(yc, yd))
    d1 = swap(both(*y1), n, 1)
    kb = [(x0[0], 0), (x1[0], 0), (cx1, 0), (x2[0], 0), (cxo, 0), (y0[0], 0), (d0, 0), (y1[0], 0), (d1, 0)]
    vb = [(x0[1], 0), (x1[1], 0), (cx1, 1), (x2[1], 0), (cxo, 1), (y0[1], 0), (d0, 1), (y1[1], 0), (d1, 1)]
    return kb, vb


def gather_y(terms, n):
    tx0, tx1, tcx1, tx2, tcxo, ty0, td0, ty1, td1 = terms
    f32 = jnp.float32
    bf16 = jnp.bfloat16
    ys0 = (ty0.astype(f32) + swap(td0, n, 1).astype(f32)).astype(bf16)
    ys1 = (ty1.astype(f32) + swap(td1, n, 1).astype(f32)).astype(bf16)
    return ys0, ys1


def unroute(terms, ys0, ys1, n, half, core):
    tx0, tx1, tcx1, tx2, tcxo, ty0, td0, ty1, td1 = terms
    f32 = jnp.float32
    bf16 = jnp.bfloat16
    yret0 = swap(ys0, n, 2).astype(f32)
    yret1 = swap(ys1, n, 2).astype(f32)
    ro = swap(tcxo, n, 1).astype(f32)
    r1 = swap(tcx1, n, 1).astype(f32)
    zero = jnp.zeros_like(r1)
    lo = half == 0
    part2 = tx2.astype(f32) + jnp.where(core == 1, ro, zero) + jnp.where(lo, zero, yret1)
    part1 = tx1.astype(f32) + r1 + jnp.where(lo, yret1, yret0)
    part1 = part1 + shift(part2.astype(bf16), n, -PLANE).astype(f32)
    part0 = tx0.astype(f32) + jnp.where(core == 0, ro, zero) + jnp.where(lo, yret0, zero)
    part0 = part0 + shift(part1.astype(bf16), n, -PLANE).astype(f32)
    return part0.astype(bf16)


def per_device(query, normed_key_rows, value_rows, out_in, grad_out, lse):
    tok, heads_q, width = query.shape
    heads_kv = normed_key_rows.shape[1]
    groups = heads_q // heads_kv
    n = lax.axis_size("seq")
    assert HOPS == 2 * PLANE
    idx = lax.axis_index("seq")
    half = (idx % PLANE) // 2
    core = idx % 2

    q4 = query.transpose(1, 0, 2).reshape(heads_kv, groups, tok, width)
    do4 = grad_out.transpose(1, 0, 2).reshape(heads_kv, groups, tok, width)
    delta = jnp.sum(grad_out.astype(jnp.float32) * out_in.astype(jnp.float32), axis=-1)
    delta3 = delta.T.reshape(heads_kv, 1, groups * tok)
    lse3 = lse.reshape(heads_kv, 1, groups * tok)
    kb, vb = route(normed_key_rows.transpose(1, 0, 2)[None], value_rows.transpose(1, 0, 2)[None],
                   n, half, core)

    late = [3, 4, 5, 6, 7, 8]
    early = [0, 1, 2]
    modes = [0, 1, 1, 2, 1, 1, 1, 1, 1]
    dist = [0, PLANE, 3 + 2 * core, 2 * PLANE, 7 - 6 * core, 2, 1 + 2 * core, 6, 5 + 2 * core]
    terms = [None] * 18
    acc = None
    ys = None
    qb = q4
    for sel in (late, early):
        acc, out = attend_blocks(
            [modes[j] for j in sel], [dist[j] for j in sel], idx, qb, do4, lse3, delta3, acc,
            [kb[j] for j in sel] + [vb[j] for j in sel])
        for m, j in enumerate(sel):
            terms[j] = out[m]
            terms[9 + j] = out[len(sel) + m]
        if ys is None:
            ys = gather_y(terms[:9], n) + gather_y(terms[9:], n)
            ys, qb = lax.optimization_barrier((ys, q4))
    grad_k = unroute(terms[:9], ys[0], ys[1], n, half, core)
    grad_v = unroute(terms[9:], ys[2], ys[3], n, half, core)

    dq = (acc * SCALE).astype(jnp.bfloat16).reshape(heads_kv, width, groups, tok)
    grad_query = dq.transpose(3, 0, 2, 1).reshape(tok, heads_q, width)
    return (grad_query, grad_k[0].transpose(1, 0, 2), grad_v[0].transpose(1, 0, 2))


def solution(mesh):
    placed = (
        P(("dp", "seq"), None, None),
        P(("dp", "seq"), None, None),
        P(("dp", "seq"), None, None),
        P(("dp", "seq"), None, None),
        P(("dp", "seq"), None, None),
        P(None, ("dp", "seq")),
    )
    return jax.shard_map(
        per_device,
        mesh=mesh,
        in_specs=placed,
        out_specs=(
            P(("dp", "seq"), None, None),
            P(("dp", "seq"), None, None),
            P(("dp", "seq"), None, None),
        ),
        check_vma=False,
    )
```

```python
import functools

import jax
import jax.numpy as jnp
from jax import lax
from jax.experimental import pallas as pl
from jax.experimental.pallas import tpu as pltpu
from jax.sharding import PartitionSpec as P

WINDOW = 1024
HOPS = 8
PLANE = 4
HEADS_PER_STEP = 4

SCALE = 168.0 ** (-0.5)


def shift(x, n, distance):
    pairs = [(i, i + distance) for i in range(n) if 0 <= i + distance < n]
    return lax.ppermute(x, "seq", pairs)


def swap(x, n, bit):
    return lax.ppermute(x, "seq", [(i, i ^ bit) for i in range(n)])


def one_way(x, n, bit, side):
    pairs = [(i, i ^ bit) for i in range(n) if (i & bit) == side]
    return lax.ppermute(x, "seq", pairs)


def _blocks_kernel(modes, has_acc, valid_ref, q_ref, do_ref, lse_ref, delta_ref, *refs):
    nb = len(modes)
    if has_acc:
        acc_ref = refs[0]
        refs = refs[1:]
    k_refs = refs[:nb]
    v_refs = refs[nb:2 * nb]
    dq_ref = refs[2 * nb]
    dk_refs = refs[2 * nb + 1:3 * nb + 1]
    dv_refs = refs[3 * nb + 1:]
    gb, grp, tok, width = q_ref.shape
    rows = grp * tok
    kk = lax.broadcasted_iota(jnp.int32, (tok, rows), 0)
    tt = lax.broadcasted_iota(jnp.int32, (tok, rows), 1) % tok
    causal = kk <= tt
    strict = kk > tt
    for g in range(gb):
        q = q_ref[g].reshape(rows, width)
        do = do_ref[g].reshape(rows, width)
        lse = lse_ref[g]
        delta = delta_ref[g]
        if has_acc:
            dq = acc_ref[g]
        else:
            dq = jnp.zeros((width, rows), jnp.float32)
        for b, mode in enumerate(modes):
            k = k_refs[b][0, g]
            v = v_refs[b][0, g]
            off = jnp.where(valid_ref[b] > 0, 0.0, 1e30).astype(jnp.float32)
            s = lax.dot_general(k, q, (((1,), (1,)), ((), ())), preferred_element_type=jnp.float32)
            e = jnp.exp(s * SCALE - lse - off)
            if mode == 0:
                p = jnp.where(causal, e, 0.0)
            elif mode == 2:
                p = jnp.where(strict, e, 0.0)
            else:
                p = e
            dp = lax.dot_general(v, do, (((1,), (1,)), ((), ())), preferred_element_type=jnp.float32)
            ds = p * (dp - delta)
            pb = p.astype(jnp.bfloat16)
            dsb = ds.astype(jnp.bfloat16)
            dv = jnp.dot(pb, do, preferred_element_type=jnp.float32)
            dk = jnp.dot(dsb, q, preferred_element_type=jnp.float32) * SCALE
            dq = dq + lax.dot_general(k, dsb, (((0,), (0,)), ((), ())), preferred_element_type=jnp.float32)
            dk_refs[b][0, g] = dk.astype(jnp.bfloat16)
            dv_refs[b][0, g] = dv.astype(jnp.bfloat16)
        dq_ref[g] = dq


def attend_blocks(modes, dist, idx, q4, do4, lse3, delta3, acc, kvs):
    nh, grp, tok, width = q4.shape
    gb = HEADS_PER_STEP
    nb = len(modes)
    valid = jnp.stack([(idx >= d).astype(jnp.int32) for d in dist])
    hspec = pl.BlockSpec((gb, grp, tok, width), lambda i, v: (i, 0, 0, 0))
    tspec = pl.BlockSpec((gb, width, grp * tok), lambda i, v: (i, 0, 0))
    rspec = pl.BlockSpec((gb, 1, grp * tok), lambda i, v: (i, 0, 0))
    kvspec = pl.BlockSpec((1, gb, tok, width), lambda i, v: (0, i, 0, 0))
    accs = [] if acc is None else [acc]
    out_shape = [jax.ShapeDtypeStruct((nh, width, grp * tok), jnp.float32)]
    out_shape += [jax.ShapeDtypeStruct(kv.shape, jnp.bfloat16) for kv in kvs]
    grid_spec = pltpu.PrefetchScalarGridSpec(
        num_scalar_prefetch=1,
        grid=(nh // gb,),
        in_specs=[hspec, hspec, rspec, rspec] + [tspec] * len(accs) + [kvspec] * (2 * nb),
        out_specs=[tspec] + [kvspec] * (2 * nb),
    )
    scores = nh * grp * tok * tok * nb
    cost = pl.CostEstimate(
        flops=10 * scores * width,
        transcendentals=scores,
        bytes_accessed=(2 + 2 * len(accs)) * q4.size * 2 + 2 * sum(kv.size for kv in kvs) * 2,
    )
    outs = pl.pallas_call(
        functools.partial(_blocks_kernel, tuple(modes), acc is not None),
        grid_spec=grid_spec,
        out_shape=out_shape,
        cost_estimate=cost,
        compiler_params=pltpu.CompilerParams(dimension_semantics=("arbitrary",)),
    )(valid, q4, do4, lse3, delta3, *accs, *kvs)
    return outs[0], list(outs[1:])


def route(x0, n, half, core):
    x1 = shift(x0, n, PLANE)
    ya = one_way(x0, n, 2, 0)
    cx1 = swap(x1, n, 1)
    yb = one_way(x1, n, 2, 2)
    x2 = shift(x1, n, PLANE)
    ca = one_way(x0, n, 1, 0)
    cb = one_way(x2, n, 1, 1)
    yc = one_way(x1, n, 2, 0)
    yd = one_way(x2, n, 2, 2)
    y0 = jnp.where(half == 1, ya, yb)
    d0 = swap(y0, n, 1)
    cxo = jnp.where(core == 1, ca, cb)
    y1 = jnp.where(half == 1, yc, yd)
    d1 = swap(y1, n, 1)
    return [x0, x1, cx1, x2, cxo, y0, d0, y1, d1]


def gather_y(terms, n):
    tx0, tx1, tcx1, tx2, tcxo, ty0, td0, ty1, td1 = terms
    f32 = jnp.float32
    bf16 = jnp.bfloat16
    ys0 = (ty0.astype(f32) + swap(td0, n, 1).astype(f32)).astype(bf16)
    ys1 = (ty1.astype(f32) + swap(td1, n, 1).astype(f32)).astype(bf16)
    return ys0, ys1


def unroute(terms, ys0, ys1, n, half, core):
    tx0, tx1, tcx1, tx2, tcxo, ty0, td0, ty1, td1 = terms
    f32 = jnp.float32
    bf16 = jnp.bfloat16
    yret0 = swap(ys0, n, 2).astype(f32)
    yret1 = swap(ys1, n, 2).astype(f32)
    ro = swap(tcxo, n, 1).astype(f32)
    r1 = swap(tcx1, n, 1).astype(f32)
    zero = jnp.zeros_like(r1)
    lo = half == 0
    part2 = tx2.astype(f32) + jnp.where(core == 1, ro, zero) + jnp.where(lo, zero, yret1)
    part1 = tx1.astype(f32) + r1 + jnp.where(lo, yret1, yret0)
    part1 = part1 + shift(part2.astype(bf16), n, -PLANE).astype(f32)
    part0 = tx0.astype(f32) + jnp.where(core == 0, ro, zero) + jnp.where(lo, yret0, zero)
    last = shift(part1.astype(bf16)[0].transpose(1, 0, 2), n, -PLANE)
    return (part0[0].transpose(1, 0, 2) + last.astype(f32)).astype(bf16)


def per_device(query, normed_key_rows, value_rows, out_in, grad_out, lse):
    tok, heads_q, width = query.shape
    heads_kv = normed_key_rows.shape[1]
    groups = heads_q // heads_kv
    n = lax.axis_size("seq")
    assert HOPS == 2 * PLANE
    idx = lax.axis_index("seq")
    half = (idx % PLANE) // 2
    core = idx % 2

    q4 = query.transpose(1, 0, 2).reshape(heads_kv, groups, tok, width)
    do4 = grad_out.transpose(1, 0, 2).reshape(heads_kv, groups, tok, width)
    delta = jnp.sum(grad_out.astype(jnp.float32) * out_in.astype(jnp.float32), axis=-1)
    delta3 = delta.T.reshape(heads_kv, 1, groups * tok)
    lse3 = lse.reshape(heads_kv, 1, groups * tok)
    kb = route(normed_key_rows.transpose(1, 0, 2)[None], n, half, core)
    vb = route(value_rows.transpose(1, 0, 2)[None], n, half, core)

    late = [3, 4, 5, 6, 7, 8]
    early = [0, 1, 2]
    modes = [0, 1, 1, 2, 1, 1, 1, 1, 1]
    dist = [0, PLANE, 3 + 2 * core, 2 * PLANE, 7 - 6 * core, 2, 1 + 2 * core, 6, 5 + 2 * core]
    terms = [None] * 18
    acc = None
    ys = None
    qb = q4
    for sel in (late, early):
        acc, out = attend_blocks(
            [modes[j] for j in sel], [dist[j] for j in sel], idx, qb, do4, lse3, delta3, acc,
            [kb[j] for j in sel] + [vb[j] for j in sel])
        for m, j in enumerate(sel):
            terms[j] = out[m]
            terms[9 + j] = out[len(sel) + m]
        if ys is None:
            ys = gather_y(terms[:9], n) + gather_y(terms[9:], n)
            ys, qb = lax.optimization_barrier((ys, q4))
    grad_k = unroute(terms[:9], ys[0], ys[1], n, half, core)
    grad_v = unroute(terms[9:], ys[2], ys[3], n, half, core)

    dq = (acc * SCALE).astype(jnp.bfloat16).reshape(heads_kv, width, groups, tok)
    grad_query = dq.transpose(3, 0, 2, 1).reshape(tok, heads_q, width)
    return (grad_query, grad_k, grad_v)


def solution(mesh):
    placed = (
        P(("dp", "seq"), None, None),
        P(("dp", "seq"), None, None),
        P(("dp", "seq"), None, None),
        P(("dp", "seq"), None, None),
        P(("dp", "seq"), None, None),
        P(None, ("dp", "seq")),
    )
    return jax.shard_map(
        per_device,
        mesh=mesh,
        in_specs=placed,
        out_specs=(
            P(("dp", "seq"), None, None),
            P(("dp", "seq"), None, None),
            P(("dp", "seq"), None, None),
        ),
        check_vma=False,
    )
```

```python
import functools

import jax
import jax.numpy as jnp
from jax import lax
from jax.experimental import pallas as pl
from jax.experimental.pallas import tpu as pltpu
from jax.sharding import PartitionSpec as P

WINDOW = 1024
HOPS = 8
PLANE = 4
HEADS_PER_STEP = 4

SCALE = 168.0 ** (-0.5)


def shift(x, n, distance):
    pairs = [(i, i + distance) for i in range(n) if 0 <= i + distance < n]
    return lax.ppermute(x, "seq", pairs)


def swap(x, n, bit):
    return lax.ppermute(x, "seq", [(i, i ^ bit) for i in range(n)])


def one_way(x, n, bit, side):
    pairs = [(i, i ^ bit) for i in range(n) if (i & bit) == side]
    return lax.ppermute(x, "seq", pairs)


def _blocks_kernel(modes, has_acc, valid_ref, q_ref, do_ref, lse_ref, delta_ref, *refs):
    nb = len(modes)
    if has_acc:
        acc_ref = refs[0]
        refs = refs[1:]
    k_refs = refs[:nb]
    v_refs = refs[nb:2 * nb]
    dq_ref = refs[2 * nb]
    dk_refs = refs[2 * nb + 1:3 * nb + 1]
    dv_refs = refs[3 * nb + 1:]
    gb, grp, tok, width = q_ref.shape
    rows = grp * tok
    kk = lax.broadcasted_iota(jnp.int32, (tok, rows), 0)
    tt = lax.broadcasted_iota(jnp.int32, (tok, rows), 1) % tok
    causal = kk <= tt
    strict = kk > tt
    for g in range(gb):
        q = q_ref[g].reshape(rows, width)
        do = do_ref[g].reshape(rows, width)
        lse = lse_ref[g]
        delta = delta_ref[g]
        if has_acc:
            dq = acc_ref[g]
        else:
            dq = jnp.zeros((width, rows), jnp.float32)
        for b, mode in enumerate(modes):
            k = k_refs[b][0, g]
            v = v_refs[b][0, g]
            off = jnp.where(valid_ref[b] > 0, 0.0, 1e30).astype(jnp.float32)
            s = lax.dot_general(k, q, (((1,), (1,)), ((), ())), preferred_element_type=jnp.float32)
            e = jnp.exp(s * SCALE - (lse + off))
            if mode == 0:
                p = jnp.where(causal, e, 0.0)
            elif mode == 2:
                p = jnp.where(strict, e, 0.0)
            else:
                p = e
            dp = lax.dot_general(v, do, (((1,), (1,)), ((), ())), preferred_element_type=jnp.float32)
            ds = p * (dp - delta)
            pb = p.astype(jnp.bfloat16)
            dsb = ds.astype(jnp.bfloat16)
            dv = jnp.dot(pb, do, preferred_element_type=jnp.float32)
            dk = jnp.dot(dsb, q, preferred_element_type=jnp.float32) * SCALE
            dq = dq + lax.dot_general(k, dsb, (((0,), (0,)), ((), ())), preferred_element_type=jnp.float32)
            dk_refs[b][0, g] = dk.astype(jnp.bfloat16)
            dv_refs[b][0, g] = dv.astype(jnp.bfloat16)
        dq_ref[g] = dq


def attend_blocks(modes, dist, idx, q4, do4, lse3, delta3, acc, kvs):
    nh, grp, tok, width = q4.shape
    gb = HEADS_PER_STEP
    nb = len(modes)
    valid = jnp.stack([(idx >= d).astype(jnp.int32) for d in dist])
    hspec = pl.BlockSpec((gb, grp, tok, width), lambda i, v: (i, 0, 0, 0))
    tspec = pl.BlockSpec((gb, width, grp * tok), lambda i, v: (i, 0, 0))
    rspec = pl.BlockSpec((gb, 1, grp * tok), lambda i, v: (i, 0, 0))
    kvspec = pl.BlockSpec((1, gb, tok, width), lambda i, v: (0, i, 0, 0))
    accs = [] if acc is None else [acc]
    out_shape = [jax.ShapeDtypeStruct((nh, width, grp * tok), jnp.float32)]
    out_shape += [jax.ShapeDtypeStruct(kv.shape, jnp.bfloat16) for kv in kvs]
    grid_spec = pltpu.PrefetchScalarGridSpec(
        num_scalar_prefetch=1,
        grid=(nh // gb,),
        in_specs=[hspec, hspec, rspec, rspec] + [tspec] * len(accs) + [kvspec] * (2 * nb),
        out_specs=[tspec] + [kvspec] * (2 * nb),
    )
    scores = nh * grp * tok * tok * nb
    cost = pl.CostEstimate(
        flops=10 * scores * width,
        transcendentals=scores,
        bytes_accessed=(2 + 2 * len(accs)) * q4.size * 2 + 2 * sum(kv.size for kv in kvs) * 2,
    )
    outs = pl.pallas_call(
        functools.partial(_blocks_kernel, tuple(modes), acc is not None),
        grid_spec=grid_spec,
        out_shape=out_shape,
        cost_estimate=cost,
        compiler_params=pltpu.CompilerParams(dimension_semantics=("arbitrary",)),
    )(valid, q4, do4, lse3, delta3, *accs, *kvs)
    return outs[0], list(outs[1:])


def route(x0, n, half, core):
    x1 = shift(x0, n, PLANE)
    ya = one_way(x0, n, 2, 0)
    cx1 = swap(x1, n, 1)
    yb = one_way(x1, n, 2, 2)
    x2 = shift(x1, n, PLANE)
    ca = one_way(x0, n, 1, 0)
    cb = one_way(x2, n, 1, 1)
    yc = one_way(x1, n, 2, 0)
    yd = one_way(x2, n, 2, 2)
    y0 = jnp.where(half == 1, ya, yb)
    d0 = swap(y0, n, 1)
    cxo = jnp.where(core == 1, ca, cb)
    y1 = jnp.where(half == 1, yc, yd)
    d1 = swap(y1, n, 1)
    return [x0, x1, cx1, x2, cxo, y0, d0, y1, d1]


def gather_y(terms, n):
    tx0, tx1, tcx1, tx2, tcxo, ty0, td0, ty1, td1 = terms
    f32 = jnp.float32
    bf16 = jnp.bfloat16
    ys0 = (ty0.astype(f32) + swap(td0, n, 1).astype(f32)).astype(bf16)
    ys1 = (ty1.astype(f32) + swap(td1, n, 1).astype(f32)).astype(bf16)
    return ys0, ys1


def unroute(terms, ys0, ys1, n, half, core):
    tx0, tx1, tcx1, tx2, tcxo, ty0, td0, ty1, td1 = terms
    f32 = jnp.float32
    bf16 = jnp.bfloat16
    yret0 = swap(ys0, n, 2).astype(f32)
    yret1 = swap(ys1, n, 2).astype(f32)
    ro = swap(tcxo, n, 1).astype(f32)
    r1 = swap(tcx1, n, 1).astype(f32)
    zero = jnp.zeros_like(r1)
    lo = half == 0
    part2 = tx2.astype(f32) + jnp.where(core == 1, ro, zero) + jnp.where(lo, zero, yret1)
    part1 = tx1.astype(f32) + r1 + jnp.where(lo, yret1, yret0)
    part1 = part1 + shift(part2.astype(bf16), n, -PLANE).astype(f32)
    part0 = tx0.astype(f32) + jnp.where(core == 0, ro, zero) + jnp.where(lo, yret0, zero)
    last = shift(part1.astype(bf16)[0].transpose(1, 0, 2), n, -PLANE)
    return (part0[0].transpose(1, 0, 2) + last.astype(f32)).astype(bf16)


def per_device(query, normed_key_rows, value_rows, out_in, grad_out, lse):
    tok, heads_q, width = query.shape
    heads_kv = normed_key_rows.shape[1]
    groups = heads_q // heads_kv
    n = lax.axis_size("seq")
    assert HOPS == 2 * PLANE
    idx = lax.axis_index("seq")
    half = (idx % PLANE) // 2
    core = idx % 2

    q4 = query.transpose(1, 0, 2).reshape(heads_kv, groups, tok, width)
    do4 = grad_out.transpose(1, 0, 2).reshape(heads_kv, groups, tok, width)
    delta = jnp.sum(grad_out.astype(jnp.float32) * out_in.astype(jnp.float32), axis=-1)
    delta3 = delta.T.reshape(heads_kv, 1, groups * tok)
    lse3 = lse.reshape(heads_kv, 1, groups * tok)
    kb = route(normed_key_rows.transpose(1, 0, 2)[None], n, half, core)
    vb = route(value_rows.transpose(1, 0, 2)[None], n, half, core)

    late = [3, 4, 5, 6, 7, 8]
    early = [0, 1, 2]
    modes = [0, 1, 1, 2, 1, 1, 1, 1, 1]
    dist = [0, PLANE, 3 + 2 * core, 2 * PLANE, 7 - 6 * core, 2, 1 + 2 * core, 6, 5 + 2 * core]
    terms = [None] * 18
    acc = None
    ys = None
    qb = q4
    for sel in (late, early):
        acc, out = attend_blocks(
            [modes[j] for j in sel], [dist[j] for j in sel], idx, qb, do4, lse3, delta3, acc,
            [kb[j] for j in sel] + [vb[j] for j in sel])
        for m, j in enumerate(sel):
            terms[j] = out[m]
            terms[9 + j] = out[len(sel) + m]
        if ys is None:
            ys = gather_y(terms[:9], n) + gather_y(terms[9:], n)
            ys, qb = lax.optimization_barrier((ys, q4))
    grad_k = unroute(terms[:9], ys[0], ys[1], n, half, core)
    grad_v = unroute(terms[9:], ys[2], ys[3], n, half, core)

    dq = (acc * SCALE).astype(jnp.bfloat16).reshape(heads_kv, width, groups, tok)
    grad_query = dq.transpose(3, 0, 2, 1).reshape(tok, heads_q, width)
    return (grad_query, grad_k, grad_v)


def solution(mesh):
    placed = (
        P(("dp", "seq"), None, None),
        P(("dp", "seq"), None, None),
        P(("dp", "seq"), None, None),
        P(("dp", "seq"), None, None),
        P(("dp", "seq"), None, None),
        P(None, ("dp", "seq")),
    )
    return jax.shard_map(
        per_device,
        mesh=mesh,
        in_specs=placed,
        out_specs=(
            P(("dp", "seq"), None, None),
            P(("dp", "seq"), None, None),
            P(("dp", "seq"), None, None),
        ),
        check_vma=False,
    )
```

```python
import functools

import jax
import jax.numpy as jnp
from jax import lax
from jax.experimental import pallas as pl
from jax.experimental.pallas import tpu as pltpu
from jax.sharding import PartitionSpec as P

WINDOW = 1024
HOPS = 8
PLANE = 4
HEADS_PER_STEP = 8

SCALE = 168.0 ** (-0.5)


def shift(x, n, distance):
    pairs = [(i, i + distance) for i in range(n) if 0 <= i + distance < n]
    return lax.ppermute(x, "seq", pairs)


def swap(x, n, bit):
    return lax.ppermute(x, "seq", [(i, i ^ bit) for i in range(n)])


def one_way(x, n, bit, side):
    pairs = [(i, i ^ bit) for i in range(n) if (i & bit) == side]
    return lax.ppermute(x, "seq", pairs)


def _blocks_kernel(modes, has_acc, valid_ref, q_ref, do_ref, lse_ref, delta_ref, *refs):
    nb = len(modes)
    if has_acc:
        acc_ref = refs[0]
        refs = refs[1:]
    k_refs = refs[:nb]
    v_refs = refs[nb:2 * nb]
    dq_ref = refs[2 * nb]
    dk_refs = refs[2 * nb + 1:3 * nb + 1]
    dv_refs = refs[3 * nb + 1:]
    gb, grp, tok, width = q_ref.shape
    rows = grp * tok
    kk = lax.broadcasted_iota(jnp.int32, (tok, rows), 0)
    tt = lax.broadcasted_iota(jnp.int32, (tok, rows), 1) % tok
    causal = kk <= tt
    strict = kk > tt
    for g in range(gb):
        q = q_ref[g].reshape(rows, width)
        do = do_ref[g].reshape(rows, width)
        lse = lse_ref[g]
        delta = delta_ref[g]
        if has_acc:
            dq = acc_ref[g]
        else:
            dq = jnp.zeros((width, rows), jnp.float32)
        for b, mode in enumerate(modes):
            k = k_refs[b][0, g]
            v = v_refs[b][0, g]
            off = jnp.where(valid_ref[b] > 0, 0.0, 1e30).astype(jnp.float32)
            s = lax.dot_general(k, q, (((1,), (1,)), ((), ())), preferred_element_type=jnp.float32)
            e = jnp.exp(s * SCALE - (lse + off))
            if mode == 0:
                p = jnp.where(causal, e, 0.0)
            elif mode == 2:
                p = jnp.where(strict, e, 0.0)
            else:
                p = e
            dp = lax.dot_general(v, do, (((1,), (1,)), ((), ())), preferred_element_type=jnp.float32)
            ds = p * (dp - delta)
            pb = p.astype(jnp.bfloat16)
            dsb = ds.astype(jnp.bfloat16)
            dv = jnp.dot(pb, do, preferred_element_type=jnp.float32)
            dk = jnp.dot(dsb, q, preferred_element_type=jnp.float32) * SCALE
            dq = dq + lax.dot_general(k, dsb, (((0,), (0,)), ((), ())), preferred_element_type=jnp.float32)
            dk_refs[b][0, g] = dk.astype(jnp.bfloat16)
            dv_refs[b][0, g] = dv.astype(jnp.bfloat16)
        dq_ref[g] = dq


def attend_blocks(modes, dist, idx, q4, do4, lse3, delta3, acc, kvs):
    nh, grp, tok, width = q4.shape
    gb = HEADS_PER_STEP
    nb = len(modes)
    valid = jnp.stack([(idx >= d).astype(jnp.int32) for d in dist])
    hspec = pl.BlockSpec((gb, grp, tok, width), lambda i, v: (i, 0, 0, 0))
    tspec = pl.BlockSpec((gb, width, grp * tok), lambda i, v: (i, 0, 0))
    rspec = pl.BlockSpec((gb, 1, grp * tok), lambda i, v: (i, 0, 0))
    kvspec = pl.BlockSpec((1, gb, tok, width), lambda i, v: (0, i, 0, 0))
    accs = [] if acc is None else [acc]
    out_shape = [jax.ShapeDtypeStruct((nh, width, grp * tok), jnp.float32)]
    out_shape += [jax.ShapeDtypeStruct(kv.shape, jnp.bfloat16) for kv in kvs]
    grid_spec = pltpu.PrefetchScalarGridSpec(
        num_scalar_prefetch=1,
        grid=(nh // gb,),
        in_specs=[hspec, hspec, rspec, rspec] + [tspec] * len(accs) + [kvspec] * (2 * nb),
        out_specs=[tspec] + [kvspec] * (2 * nb),
    )
    scores = nh * grp * tok * tok * nb
    cost = pl.CostEstimate(
        flops=10 * scores * width,
        transcendentals=scores,
        bytes_accessed=(2 + 2 * len(accs)) * q4.size * 2 + 2 * sum(kv.size for kv in kvs) * 2,
    )
    outs = pl.pallas_call(
        functools.partial(_blocks_kernel, tuple(modes), acc is not None),
        grid_spec=grid_spec,
        out_shape=out_shape,
        cost_estimate=cost,
        compiler_params=pltpu.CompilerParams(dimension_semantics=("arbitrary",)),
    )(valid, q4, do4, lse3, delta3, *accs, *kvs)
    return outs[0], list(outs[1:])


def route(x0, n, half, core):
    x1 = shift(x0, n, PLANE)
    ya = one_way(x0, n, 2, 0)
    cx1 = swap(x1, n, 1)
    yb = one_way(x1, n, 2, 2)
    x2 = shift(x1, n, PLANE)
    ca = one_way(x0, n, 1, 0)
    cb = one_way(x2, n, 1, 1)
    yc = one_way(x1, n, 2, 0)
    yd = one_way(x2, n, 2, 2)
    y0 = jnp.where(half == 1, ya, yb)
    d0 = swap(y0, n, 1)
    cxo = jnp.where(core == 1, ca, cb)
    y1 = jnp.where(half == 1, yc, yd)
    d1 = swap(y1, n, 1)
    return [x0, x1, cx1, x2, cxo, y0, d0, y1, d1]


def gather_y(terms, n):
    tx0, tx1, tcx1, tx2, tcxo, ty0, td0, ty1, td1 = terms
    f32 = jnp.float32
    bf16 = jnp.bfloat16
    ys0 = (ty0.astype(f32) + swap(td0, n, 1).astype(f32)).astype(bf16)
    ys1 = (ty1.astype(f32) + swap(td1, n, 1).astype(f32)).astype(bf16)
    return ys0, ys1


def unroute(terms, ys0, ys1, n, half, core):
    tx0, tx1, tcx1, tx2, tcxo, ty0, td0, ty1, td1 = terms
    f32 = jnp.float32
    bf16 = jnp.bfloat16
    yret0 = swap(ys0, n, 2).astype(f32)
    yret1 = swap(ys1, n, 2).astype(f32)
    ro = swap(tcxo, n, 1).astype(f32)
    r1 = swap(tcx1, n, 1).astype(f32)
    zero = jnp.zeros_like(r1)
    lo = half == 0
    part2 = tx2.astype(f32) + jnp.where(core == 1, ro, zero) + jnp.where(lo, zero, yret1)
    part1 = tx1.astype(f32) + r1 + jnp.where(lo, yret1, yret0)
    part1 = part1 + shift(part2.astype(bf16), n, -PLANE).astype(f32)
    part0 = tx0.astype(f32) + jnp.where(core == 0, ro, zero) + jnp.where(lo, yret0, zero)
    last = shift(part1.astype(bf16)[0].transpose(1, 0, 2), n, -PLANE)
    return (part0[0].transpose(1, 0, 2) + last.astype(f32)).astype(bf16)


def per_device(query, normed_key_rows, value_rows, out_in, grad_out, lse):
    tok, heads_q, width = query.shape
    heads_kv = normed_key_rows.shape[1]
    groups = heads_q // heads_kv
    n = lax.axis_size("seq")
    assert HOPS == 2 * PLANE
    idx = lax.axis_index("seq")
    half = (idx % PLANE) // 2
    core = idx % 2

    q4 = query.transpose(1, 0, 2).reshape(heads_kv, groups, tok, width)
    do4 = grad_out.transpose(1, 0, 2).reshape(heads_kv, groups, tok, width)
    delta = jnp.sum(grad_out.astype(jnp.float32) * out_in.astype(jnp.float32), axis=-1)
    delta3 = delta.T.reshape(heads_kv, 1, groups * tok)
    lse3 = lse.reshape(heads_kv, 1, groups * tok)
    kb = route(normed_key_rows.transpose(1, 0, 2)[None], n, half, core)
    vb = route(value_rows.transpose(1, 0, 2)[None], n, half, core)

    late = [3, 4, 5, 6, 7, 8]
    early = [0, 1, 2]
    modes = [0, 1, 1, 2, 1, 1, 1, 1, 1]
    dist = [0, PLANE, 3 + 2 * core, 2 * PLANE, 7 - 6 * core, 2, 1 + 2 * core, 6, 5 + 2 * core]
    terms = [None] * 18
    acc = None
    ys = None
    qb = q4
    for sel in (late, early):
        acc, out = attend_blocks(
            [modes[j] for j in sel], [dist[j] for j in sel], idx, qb, do4, lse3, delta3, acc,
            [kb[j] for j in sel] + [vb[j] for j in sel])
        for m, j in enumerate(sel):
            terms[j] = out[m]
            terms[9 + j] = out[len(sel) + m]
        if ys is None:
            ys = gather_y(terms[:9], n) + gather_y(terms[9:], n)
            ys, qb = lax.optimization_barrier((ys, q4))
    grad_k = unroute(terms[:9], ys[0], ys[1], n, half, core)
    grad_v = unroute(terms[9:], ys[2], ys[3], n, half, core)

    dq = (acc * SCALE).astype(jnp.bfloat16).reshape(heads_kv, width, groups, tok)
    grad_query = dq.transpose(3, 0, 2, 1).reshape(tok, heads_q, width)
    return (grad_query, grad_k, grad_v)


def solution(mesh):
    placed = (
        P(("dp", "seq"), None, None),
        P(("dp", "seq"), None, None),
        P(("dp", "seq"), None, None),
        P(("dp", "seq"), None, None),
        P(("dp", "seq"), None, None),
        P(None, ("dp", "seq")),
    )
    return jax.shard_map(
        per_device,
        mesh=mesh,
        in_specs=placed,
        out_specs=(
            P(("dp", "seq"), None, None),
            P(("dp", "seq"), None, None),
            P(("dp", "seq"), None, None),
        ),
        check_vma=False,
    )
```

```python
import functools

import jax
import jax.numpy as jnp
from jax import lax
from jax.experimental import pallas as pl
from jax.experimental.pallas import tpu as pltpu
from jax.sharding import PartitionSpec as P

WINDOW = 1024
HOPS = 8
PLANE = 4
HEADS_PER_STEP = 4

SCALE = 168.0 ** (-0.5)


def shift(x, n, distance):
    pairs = [(i, i + distance) for i in range(n) if 0 <= i + distance < n]
    return lax.ppermute(x, "seq", pairs)


def swap(x, n, bit):
    return lax.ppermute(x, "seq", [(i, i ^ bit) for i in range(n)])


def one_way(x, n, bit, side):
    pairs = [(i, i ^ bit) for i in range(n) if (i & bit) == side]
    return lax.ppermute(x, "seq", pairs)


def _blocks_kernel(modes, has_acc, valid_ref, q_ref, do_ref, lse_ref, delta_ref, *refs):
    nb = len(modes)
    if has_acc:
        acc_ref = refs[0]
        refs = refs[1:]
    k_refs = refs[:nb]
    v_refs = refs[nb:2 * nb]
    dq_ref = refs[2 * nb]
    dk_refs = refs[2 * nb + 1:3 * nb + 1]
    dv_refs = refs[3 * nb + 1:]
    gb, grp, tok, width = q_ref.shape
    rows = grp * tok
    kk = lax.broadcasted_iota(jnp.int32, (tok, rows), 0)
    tt = lax.broadcasted_iota(jnp.int32, (tok, rows), 1) % tok
    causal = kk <= tt
    strict = kk > tt
    for g in range(gb):
        q = q_ref[g].reshape(rows, width)
        do = do_ref[g].reshape(rows, width)
        lse = lse_ref[g]
        delta = delta_ref[g]
        if has_acc:
            dq = acc_ref[g]
        else:
            dq = jnp.zeros((width, rows), jnp.float32)
        for b, mode in enumerate(modes):
            k = k_refs[b][0, g]
            v = v_refs[b][0, g]
            off = jnp.where(valid_ref[b] > 0, 0.0, 1e30).astype(jnp.float32)
            s = lax.dot_general(k, q, (((1,), (1,)), ((), ())), preferred_element_type=jnp.float32)
            e = jnp.exp(s * SCALE - (lse + off))
            if mode == 0:
                p = jnp.where(causal, e, 0.0)
            elif mode == 2:
                p = jnp.where(strict, e, 0.0)
            else:
                p = e
            dp = lax.dot_general(v, do, (((1,), (1,)), ((), ())), preferred_element_type=jnp.float32)
            ds = p * (dp - delta)
            pb = p.astype(jnp.bfloat16)
            dsb = ds.astype(jnp.bfloat16)
            dv = jnp.dot(pb, do, preferred_element_type=jnp.float32)
            dk = jnp.dot(dsb, q, preferred_element_type=jnp.float32) * SCALE
            dq = dq + lax.dot_general(k, dsb, (((0,), (0,)), ((), ())), preferred_element_type=jnp.float32)
            dk_refs[b][0, g] = dk.astype(jnp.bfloat16)
            dv_refs[b][0, g] = dv.astype(jnp.bfloat16)
        dq_ref[g] = dq


def attend_blocks(modes, dist, idx, q4, do4, lse3, delta3, acc, kvs):
    nh, grp, tok, width = q4.shape
    gb = HEADS_PER_STEP
    nb = len(modes)
    valid = jnp.stack([(idx >= d).astype(jnp.int32) for d in dist])
    hspec = pl.BlockSpec((gb, grp, tok, width), lambda i, v: (i, 0, 0, 0))
    tspec = pl.BlockSpec((gb, width, grp * tok), lambda i, v: (i, 0, 0))
    rspec = pl.BlockSpec((gb, 1, grp * tok), lambda i, v: (i, 0, 0))
    kvspec = pl.BlockSpec((1, gb, tok, width), lambda i, v: (0, i, 0, 0))
    accs = [] if acc is None else [acc]
    out_shape = [jax.ShapeDtypeStruct((nh, width, grp * tok), jnp.float32)]
    out_shape += [jax.ShapeDtypeStruct(kv.shape, jnp.bfloat16) for kv in kvs]
    grid_spec = pltpu.PrefetchScalarGridSpec(
        num_scalar_prefetch=1,
        grid=(nh // gb,),
        in_specs=[hspec, hspec, rspec, rspec] + [tspec] * len(accs) + [kvspec] * (2 * nb),
        out_specs=[tspec] + [kvspec] * (2 * nb),
    )
    scores = nh * grp * tok * tok * nb
    cost = pl.CostEstimate(
        flops=10 * scores * width,
        transcendentals=scores,
        bytes_accessed=(2 + 2 * len(accs)) * q4.size * 2 + 2 * sum(kv.size for kv in kvs) * 2,
    )
    outs = pl.pallas_call(
        functools.partial(_blocks_kernel, tuple(modes), acc is not None),
        grid_spec=grid_spec,
        out_shape=out_shape,
        cost_estimate=cost,
        compiler_params=pltpu.CompilerParams(dimension_semantics=("arbitrary",)),
    )(valid, q4, do4, lse3, delta3, *accs, *kvs)
    return outs[0], list(outs[1:])


def route(x0, n, half, core):
    x1 = shift(x0, n, PLANE)
    ya = one_way(x0, n, 2, 0)
    cx1 = swap(x1, n, 1)
    yb = one_way(x1, n, 2, 2)
    x2 = shift(x1, n, PLANE)
    ca = one_way(x0, n, 1, 0)
    cb = one_way(x2, n, 1, 1)
    yc = one_way(x1, n, 2, 0)
    yd = one_way(x2, n, 2, 2)
    y0 = jnp.where(half == 1, ya, yb)
    d0 = swap(y0, n, 1)
    cxo = jnp.where(core == 1, ca, cb)
    return [x0, x1, cx1, x2, cxo, y0, d0, yc, yd]


def gather_y(terms, n):
    tx0, tx1, tcx1, tx2, tcxo, ty0, td0, ty1, td1 = terms
    f32 = jnp.float32
    bf16 = jnp.bfloat16
    ys0 = (ty0.astype(f32) + swap(td0, n, 1).astype(f32)).astype(bf16)
    ys1 = (ty1.astype(f32) + swap(td1, n, 1).astype(f32)).astype(bf16)
    return ys0, ys1


def unroute(terms, ys0, ys1, n, half, core):
    tx0, tx1, tcx1, tx2, tcxo, ty0, td0, ty1, td1 = terms
    f32 = jnp.float32
    bf16 = jnp.bfloat16
    yret0 = swap(ys0, n, 2).astype(f32)
    yret1 = swap(ys1, n, 2).astype(f32)
    ro = swap(tcxo, n, 1).astype(f32)
    r1 = swap(tcx1, n, 1).astype(f32)
    zero = jnp.zeros_like(r1)
    lo = half == 0
    part2 = tx2.astype(f32) + jnp.where(core == 1, ro, zero) + jnp.where(lo, zero, yret1)
    part1 = tx1.astype(f32) + r1 + jnp.where(lo, yret1, yret0)
    part1 = part1 + shift(part2.astype(bf16), n, -PLANE).astype(f32)
    part0 = tx0.astype(f32) + jnp.where(core == 0, ro, zero) + jnp.where(lo, yret0, zero)
    last = shift(part1.astype(bf16)[0].transpose(1, 0, 2), n, -PLANE)
    return (part0[0].transpose(1, 0, 2) + last.astype(f32)).astype(bf16)


def per_device(query, normed_key_rows, value_rows, out_in, grad_out, lse):
    tok, heads_q, width = query.shape
    heads_kv = normed_key_rows.shape[1]
    groups = heads_q // heads_kv
    n = lax.axis_size("seq")
    assert HOPS == 2 * PLANE
    idx = lax.axis_index("seq")
    half = (idx % PLANE) // 2
    core = idx % 2

    q4 = query.transpose(1, 0, 2).reshape(heads_kv, groups, tok, width)
    do4 = grad_out.transpose(1, 0, 2).reshape(heads_kv, groups, tok, width)
    delta = jnp.sum(grad_out.astype(jnp.float32) * out_in.astype(jnp.float32), axis=-1)
    delta3 = delta.T.reshape(heads_kv, 1, groups * tok)
    lse3 = lse.reshape(heads_kv, 1, groups * tok)
    kb = route(normed_key_rows.transpose(1, 0, 2)[None], n, half, core)
    vb = route(value_rows.transpose(1, 0, 2)[None], n, half, core)

    modes = [0, 1, 1, 2, 1, 1, 1, 1, 1]
    dist = [0, PLANE, 3 + 2 * core, 2 * PLANE, 7 - 6 * core, 2, 1 + 2 * core, 6, 5 + 2 * core]
    terms = [None] * 18

    def run(sel, acc, q):
        acc, out = attend_blocks(
            [modes[j] for j in sel], [dist[j] for j in sel], idx, q, do4, lse3, delta3, acc,
            [kb[j] for j in sel] + [vb[j] for j in sel])
        for m, j in enumerate(sel):
            terms[j] = out[m]
            terms[9 + j] = out[len(sel) + m]
        return acc

    acc = run([3, 4, 5, 6], None, q4)
    (kb[7], kb[8], vb[7], vb[8]), acc = lax.optimization_barrier(((kb[7], kb[8], vb[7], vb[8]), acc))
    for b in (kb, vb):
        b[7] = jnp.where(half == 1, b[7], b[8])
        b[8] = swap(b[7], n, 1)
    acc = run([7, 8], acc, q4)
    ys = gather_y(terms[:9], n) + gather_y(terms[9:], n)
    ys, qb = lax.optimization_barrier((ys, q4))
    acc = run([0, 1, 2], acc, qb)
    grad_k = unroute(terms[:9], ys[0], ys[1], n, half, core)
    grad_v = unroute(terms[9:], ys[2], ys[3], n, half, core)

    dq = (acc * SCALE).astype(jnp.bfloat16).reshape(heads_kv, width, groups, tok)
    grad_query = dq.transpose(3, 0, 2, 1).reshape(tok, heads_q, width)
    return (grad_query, grad_k, grad_v)


def solution(mesh):
    placed = (
        P(("dp", "seq"), None, None),
        P(("dp", "seq"), None, None),
        P(("dp", "seq"), None, None),
        P(("dp", "seq"), None, None),
        P(("dp", "seq"), None, None),
        P(None, ("dp", "seq")),
    )
    return jax.shard_map(
        per_device,
        mesh=mesh,
        in_specs=placed,
        out_specs=(
            P(("dp", "seq"), None, None),
            P(("dp", "seq"), None, None),
            P(("dp", "seq"), None, None),
        ),
        check_vma=False,
    )
```

```python
import functools

import jax
import jax.numpy as jnp
from jax import lax
from jax.experimental import pallas as pl
from jax.experimental.pallas import tpu as pltpu
from jax.sharding import PartitionSpec as P

WINDOW = 1024
HOPS = 8
PLANE = 4
HEADS_PER_STEP = 4

SCALE = 168.0 ** (-0.5)


def shift(x, n, distance):
    pairs = [(i, i + distance) for i in range(n) if 0 <= i + distance < n]
    return lax.ppermute(x, "seq", pairs)


def swap(x, n, bit):
    return lax.ppermute(x, "seq", [(i, i ^ bit) for i in range(n)])


def one_way(x, n, bit, side):
    pairs = [(i, i ^ bit) for i in range(n) if (i & bit) == side]
    return lax.ppermute(x, "seq", pairs)


def _blocks_kernel(modes, has_acc, valid_ref, q_ref, do_ref, lse_ref, delta_ref, *refs):
    nb = len(modes)
    if has_acc:
        acc_ref = refs[0]
        refs = refs[1:]
    k_refs = refs[:nb]
    v_refs = refs[nb:2 * nb]
    dq_ref = refs[2 * nb]
    dk_refs = refs[2 * nb + 1:3 * nb + 1]
    dv_refs = refs[3 * nb + 1:]
    gb, grp, tok, width = q_ref.shape
    rows = grp * tok
    kk = lax.broadcasted_iota(jnp.int32, (tok, rows), 0)
    tt = lax.broadcasted_iota(jnp.int32, (tok, rows), 1) % tok
    causal = kk <= tt
    strict = kk > tt
    for g in range(gb):
        q = q_ref[g].reshape(rows, width)
        do = do_ref[g].reshape(rows, width)
        lse = lse_ref[g]
        delta = delta_ref[g]
        if has_acc:
            dq = acc_ref[g]
        else:
            dq = jnp.zeros((width, rows), jnp.float32)
        for b, mode in enumerate(modes):
            k = k_refs[b][0, g]
            v = v_refs[b][0, g]
            off = jnp.where(valid_ref[b] > 0, 0.0, 1e30).astype(jnp.float32)
            s = lax.dot_general(k, q, (((1,), (1,)), ((), ())), preferred_element_type=jnp.float32)
            e = jnp.exp(s * SCALE - (lse + off))
            if mode == 0:
                p = jnp.where(causal, e, 0.0)
            elif mode == 2:
                p = jnp.where(strict, e, 0.0)
            else:
                p = e
            dp = lax.dot_general(v, do, (((1,), (1,)), ((), ())), preferred_element_type=jnp.float32)
            ds = p * (dp - delta)
            pb = p.astype(jnp.bfloat16)
            dsb = ds.astype(jnp.bfloat16)
            dv = jnp.dot(pb, do, preferred_element_type=jnp.float32)
            dk = jnp.dot(dsb, q, preferred_element_type=jnp.float32) * SCALE
            dq = dq + lax.dot_general(k, dsb, (((0,), (0,)), ((), ())), preferred_element_type=jnp.float32)
            dk_refs[b][0, g] = dk.astype(jnp.bfloat16)
            dv_refs[b][0, g] = dv.astype(jnp.bfloat16)
        dq_ref[g] = dq


def attend_blocks(modes, dist, idx, q4, do4, lse3, delta3, acc, kvs):
    nh, grp, tok, width = q4.shape
    gb = HEADS_PER_STEP
    nb = len(modes)
    valid = jnp.stack([(idx >= d).astype(jnp.int32) for d in dist])
    hspec = pl.BlockSpec((gb, grp, tok, width), lambda i, v: (i, 0, 0, 0))
    tspec = pl.BlockSpec((gb, width, grp * tok), lambda i, v: (i, 0, 0))
    rspec = pl.BlockSpec((gb, 1, grp * tok), lambda i, v: (i, 0, 0))
    kvspec = pl.BlockSpec((1, gb, tok, width), lambda i, v: (0, i, 0, 0))
    accs = [] if acc is None else [acc]
    out_shape = [jax.ShapeDtypeStruct((nh, width, grp * tok), jnp.float32)]
    out_shape += [jax.ShapeDtypeStruct(kv.shape, jnp.bfloat16) for kv in kvs]
    grid_spec = pltpu.PrefetchScalarGridSpec(
        num_scalar_prefetch=1,
        grid=(nh // gb,),
        in_specs=[hspec, hspec, rspec, rspec] + [tspec] * len(accs) + [kvspec] * (2 * nb),
        out_specs=[tspec] + [kvspec] * (2 * nb),
    )
    scores = nh * grp * tok * tok * nb
    cost = pl.CostEstimate(
        flops=10 * scores * width,
        transcendentals=scores,
        bytes_accessed=(2 + 2 * len(accs)) * q4.size * 2 + 2 * sum(kv.size for kv in kvs) * 2,
    )
    outs = pl.pallas_call(
        functools.partial(_blocks_kernel, tuple(modes), acc is not None),
        grid_spec=grid_spec,
        out_shape=out_shape,
        cost_estimate=cost,
        compiler_params=pltpu.CompilerParams(dimension_semantics=("arbitrary",)),
    )(valid, q4, do4, lse3, delta3, *accs, *kvs)
    return outs[0], list(outs[1:])


def route(x0, n, half, core):
    x1 = shift(x0, n, PLANE)
    ya = one_way(x0, n, 2, 0)
    cx1 = swap(x1, n, 1)
    yb = one_way(x1, n, 2, 2)
    x2 = shift(x1, n, PLANE)
    ca = one_way(x0, n, 1, 0)
    cb = one_way(x2, n, 1, 1)
    yc = one_way(x1, n, 2, 0)
    yd = one_way(x2, n, 2, 2)
    y0 = jnp.where(half == 1, ya, yb)
    d0 = swap(y0, n, 1)
    cxo = jnp.where(core == 1, ca, cb)
    y1 = jnp.where(half == 1, yc, yd)
    d1 = swap(y1, n, 1)
    return [x0, x1, cx1, x2, cxo, y0, d0, y1, d1]


def gather_y(terms, n):
    tx0, tx1, tcx1, tx2, tcxo, ty0, td0, ty1, td1 = terms
    f32 = jnp.float32
    bf16 = jnp.bfloat16
    ys0 = (ty0.astype(f32) + swap(td0, n, 1).astype(f32)).astype(bf16)
    ys1 = (ty1.astype(f32) + swap(td1, n, 1).astype(f32)).astype(bf16)
    return ys0, ys1


def unroute(terms, ys0, ys1, n, half, core):
    tx0, tx1, tcx1, tx2, tcxo, ty0, td0, ty1, td1 = terms
    f32 = jnp.float32
    bf16 = jnp.bfloat16
    yret0 = swap(ys0, n, 2).astype(f32)
    yret1 = swap(ys1, n, 2).astype(f32)
    ro = swap(tcxo, n, 1).astype(f32)
    r1 = swap(tcx1, n, 1).astype(f32)
    zero = jnp.zeros_like(r1)
    lo = half == 0
    part2 = tx2.astype(f32) + jnp.where(core == 1, ro, zero) + jnp.where(lo, zero, yret1)
    part1 = tx1.astype(f32) + r1 + jnp.where(lo, yret1, yret0)
    part1 = part1 + shift(part2.astype(bf16), n, -PLANE).astype(f32)
    part0 = tx0.astype(f32) + jnp.where(core == 0, ro, zero) + jnp.where(lo, yret0, zero)
    last = shift(part1.astype(bf16)[0].transpose(1, 0, 2), n, -PLANE)
    return (part0[0].transpose(1, 0, 2) + last.astype(f32)).astype(bf16)


def per_device(query, normed_key_rows, value_rows, out_in, grad_out, lse):
    tok, heads_q, width = query.shape
    heads_kv = normed_key_rows.shape[1]
    groups = heads_q // heads_kv
    n = lax.axis_size("seq")
    assert HOPS == 2 * PLANE
    idx = lax.axis_index("seq")
    half = (idx % PLANE) // 2
    core = idx % 2

    q4 = query.transpose(1, 0, 2).reshape(heads_kv, groups, tok, width)
    do4 = grad_out.transpose(1, 0, 2).reshape(heads_kv, groups, tok, width)
    delta = jnp.sum(grad_out.astype(jnp.float32) * out_in.astype(jnp.float32), axis=-1)
    delta3 = delta.T.reshape(heads_kv, 1, groups * tok)
    lse3 = lse.reshape(heads_kv, 1, groups * tok)
    kb = route(normed_key_rows.transpose(1, 0, 2)[None], n, half, core)
    vb = route(value_rows.transpose(1, 0, 2)[None], n, half, core)

    late = [3, 4, 5, 6, 7, 8]
    early = [0, 1, 2]
    modes = [0, 1, 1, 2, 1, 1, 1, 1, 1]
    dist = [0, PLANE, 3 + 2 * core, 2 * PLANE, 7 - 6 * core, 2, 1 + 2 * core, 6, 5 + 2 * core]
    terms = [None] * 18
    spans = (slice(0, heads_kv // 2), slice(heads_kv // 2, heads_kv))
    acc = None
    ys = None
    qb = q4
    for sel in (late, early):
        acc, out = attend_blocks(
            [modes[j] for j in sel], [dist[j] for j in sel], idx, qb, do4, lse3, delta3, acc,
            [kb[j] for j in sel] + [vb[j] for j in sel])
        for m, j in enumerate(sel):
            terms[j] = out[m]
            terms[9 + j] = out[len(sel) + m]
        if ys is None:
            ys = [gather_y([None if t is None else t[:, hs] for t in terms[base:base + 9]], n)
                  for hs in spans for base in (0, 9)]
            ys, qb = lax.optimization_barrier((ys, q4))
    grads = [unroute([t[:, hs] for t in terms[base:base + 9]], *ys[2 * i + s], n, half, core)
             for i, hs in enumerate(spans) for s, base in enumerate((0, 9))]
    grad_k = jnp.concatenate(grads[0::2], axis=1)
    grad_v = jnp.concatenate(grads[1::2], axis=1)

    dq = (acc * SCALE).astype(jnp.bfloat16).reshape(heads_kv, width, groups, tok)
    grad_query = dq.transpose(3, 0, 2, 1).reshape(tok, heads_q, width)
    return (grad_query, grad_k, grad_v)


def solution(mesh):
    placed = (
        P(("dp", "seq"), None, None),
        P(("dp", "seq"), None, None),
        P(("dp", "seq"), None, None),
        P(("dp", "seq"), None, None),
        P(("dp", "seq"), None, None),
        P(None, ("dp", "seq")),
    )
    return jax.shard_map(
        per_device,
        mesh=mesh,
        in_specs=placed,
        out_specs=(
            P(("dp", "seq"), None, None),
            P(("dp", "seq"), None, None),
            P(("dp", "seq"), None, None),
        ),
        check_vma=False,
    )
```

```python
import functools

import jax
import jax.numpy as jnp
from jax import lax
from jax.experimental import pallas as pl
from jax.experimental.pallas import tpu as pltpu
from jax.sharding import PartitionSpec as P

WINDOW = 1024
HOPS = 8
PLANE = 4
HEADS_PER_STEP = 4

SCALE = 168.0 ** (-0.5)


def shift(x, n, distance):
    pairs = [(i, i + distance) for i in range(n) if 0 <= i + distance < n]
    return lax.ppermute(x, "seq", pairs)


def swap(x, n, bit):
    return lax.ppermute(x, "seq", [(i, i ^ bit) for i in range(n)])


def one_way(x, n, bit, side):
    pairs = [(i, i ^ bit) for i in range(n) if (i & bit) == side]
    return lax.ppermute(x, "seq", pairs)


def _blocks_kernel(modes, has_acc, valid_ref, q_ref, do_ref, lse_ref, delta_ref, *refs):
    nb = len(modes)
    if has_acc:
        acc_ref = refs[0]
        refs = refs[1:]
    k_refs = refs[:nb]
    v_refs = refs[nb:2 * nb]
    dq_ref = refs[2 * nb]
    dk_refs = refs[2 * nb + 1:3 * nb + 1]
    dv_refs = refs[3 * nb + 1:]
    gb, grp, tok, width = q_ref.shape
    rows = grp * tok
    kk = lax.broadcasted_iota(jnp.int32, (tok, rows), 0)
    tt = lax.broadcasted_iota(jnp.int32, (tok, rows), 1) % tok
    causal = kk <= tt
    strict = kk > tt
    for g in range(gb):
        q = q_ref[g].reshape(rows, width)
        do = do_ref[g].reshape(rows, width)
        lse = lse_ref[g]
        delta = delta_ref[g]
        if has_acc:
            dq = acc_ref[g]
        else:
            dq = jnp.zeros((width, rows), jnp.float32)
        for b, mode in enumerate(modes):
            k = k_refs[b][0, g]
            v = v_refs[b][0, g]
            off = jnp.where(valid_ref[b] > 0, 0.0, 1e30).astype(jnp.float32)
            s = lax.dot_general(k, q, (((1,), (1,)), ((), ())), preferred_element_type=jnp.float32)
            e = jnp.exp(s * SCALE - (lse + off))
            if mode == 0:
                p = jnp.where(causal, e, 0.0)
            elif mode == 2:
                p = jnp.where(strict, e, 0.0)
            else:
                p = e
            dp = lax.dot_general(v, do, (((1,), (1,)), ((), ())), preferred_element_type=jnp.float32)
            ds = p * (dp - delta)
            pb = p.astype(jnp.bfloat16)
            dsb = ds.astype(jnp.bfloat16)
            dv = jnp.dot(pb, do, preferred_element_type=jnp.float32)
            dk = jnp.dot(dsb, q, preferred_element_type=jnp.float32) * SCALE
            dq = dq + lax.dot_general(k, dsb, (((0,), (0,)), ((), ())), preferred_element_type=jnp.float32)
            dk_refs[b][0, g] = dk.astype(jnp.bfloat16)
            dv_refs[b][0, g] = dv.astype(jnp.bfloat16)
        dq_ref[g] = dq


def attend_blocks(modes, dist, idx, q4, do4, lse3, delta3, acc, kvs):
    nh, grp, tok, width = q4.shape
    gb = HEADS_PER_STEP
    nb = len(modes)
    valid = jnp.stack([(idx >= d).astype(jnp.int32) for d in dist])
    hspec = pl.BlockSpec((gb, grp, tok, width), lambda i, v: (i, 0, 0, 0))
    tspec = pl.BlockSpec((gb, width, grp * tok), lambda i, v: (i, 0, 0))
    rspec = pl.BlockSpec((gb, 1, grp * tok), lambda i, v: (i, 0, 0))
    kvspec = pl.BlockSpec((1, gb, tok, width), lambda i, v: (0, i, 0, 0))
    accs = [] if acc is None else [acc]
    out_shape = [jax.ShapeDtypeStruct((nh, width, grp * tok), jnp.float32)]
    out_shape += [jax.ShapeDtypeStruct(kv.shape, jnp.bfloat16) for kv in kvs]
    grid_spec = pltpu.PrefetchScalarGridSpec(
        num_scalar_prefetch=1,
        grid=(nh // gb,),
        in_specs=[hspec, hspec, rspec, rspec] + [tspec] * len(accs) + [kvspec] * (2 * nb),
        out_specs=[tspec] + [kvspec] * (2 * nb),
    )
    scores = nh * grp * tok * tok * nb
    cost = pl.CostEstimate(
        flops=10 * scores * width,
        transcendentals=scores,
        bytes_accessed=(2 + 2 * len(accs)) * q4.size * 2 + 2 * sum(kv.size for kv in kvs) * 2,
    )
    outs = pl.pallas_call(
        functools.partial(_blocks_kernel, tuple(modes), acc is not None),
        grid_spec=grid_spec,
        out_shape=out_shape,
        cost_estimate=cost,
        compiler_params=pltpu.CompilerParams(dimension_semantics=("arbitrary",)),
    )(valid, q4, do4, lse3, delta3, *accs, *kvs)
    return outs[0], list(outs[1:])


def route(x0, n, half, core):
    x1 = shift(x0, n, PLANE)
    ya = one_way(x0, n, 2, 0)
    cx1 = swap(x1, n, 1)
    yb = one_way(x1, n, 2, 2)
    x2 = shift(x1, n, PLANE)
    ca = one_way(x0, n, 1, 0)
    cb = one_way(x2, n, 1, 1)
    yc = one_way(x1, n, 2, 0)
    yd = one_way(x2, n, 2, 2)
    y0 = jnp.where(half == 1, ya, yb)
    d0 = swap(y0, n, 1)
    cxo = jnp.where(core == 1, ca, cb)
    y1 = jnp.where(half == 1, yc, yd)
    d1 = swap(y1, n, 1)
    return [x0, x1, cx1, x2, cxo, y0, d0, y1, d1]


def gather_y(terms, n):
    tx0, tx1, tcx1, tx2, tcxo, ty0, td0, ty1, td1 = terms
    f32 = jnp.float32
    bf16 = jnp.bfloat16
    ys0 = (ty0.astype(f32) + swap(td0, n, 1).astype(f32)).astype(bf16)
    ys1 = (ty1.astype(f32) + swap(td1, n, 1).astype(f32)).astype(bf16)
    return ys0, ys1


def unroute(terms, ys0, ys1, n, half, core):
    tx0, tx1, tcx1, tx2, tcxo, ty0, td0, ty1, td1 = terms
    f32 = jnp.float32
    bf16 = jnp.bfloat16
    yret0 = swap(ys0, n, 2).astype(f32)
    yret1 = swap(ys1, n, 2).astype(f32)
    ro = swap(tcxo, n, 1).astype(f32)
    r1 = swap(tcx1, n, 1).astype(f32)
    zero = jnp.zeros_like(r1)
    lo = half == 0
    part2 = tx2.astype(f32) + jnp.where(core == 1, ro, zero) + jnp.where(lo, zero, yret1)
    part1 = tx1.astype(f32) + r1 + jnp.where(lo, yret1, yret0)
    part1 = part1 + shift(part2.astype(bf16), n, -PLANE).astype(f32)
    part0 = tx0.astype(f32) + jnp.where(core == 0, ro, zero) + jnp.where(lo, yret0, zero)
    last = shift(part1.astype(bf16)[0].transpose(1, 0, 2), n, -PLANE)
    return (part0[0].transpose(1, 0, 2) + last.astype(f32)).astype(bf16)


def per_device(query, normed_key_rows, value_rows, out_in, grad_out, lse):
    tok, heads_q, width = query.shape
    heads_kv = normed_key_rows.shape[1]
    groups = heads_q // heads_kv
    n = lax.axis_size("seq")
    assert HOPS == 2 * PLANE
    idx = lax.axis_index("seq")
    half = (idx % PLANE) // 2
    core = idx % 2

    q4 = query.transpose(1, 0, 2).reshape(heads_kv, groups, tok, width)
    do4 = grad_out.transpose(1, 0, 2).reshape(heads_kv, groups, tok, width)
    delta = jnp.sum(grad_out.astype(jnp.float32) * out_in.astype(jnp.float32), axis=-1)
    delta3 = delta.T.reshape(heads_kv, 1, groups * tok)
    lse3 = lse.reshape(heads_kv, 1, groups * tok)
    kb = route(normed_key_rows.transpose(1, 0, 2)[None], n, half, core)
    vb = route(value_rows.transpose(1, 0, 2)[None], n, half, core)

    late = [3, 4, 5, 6, 7, 8]
    early = [0, 1, 2]
    modes = [0, 1, 1, 2, 1, 1, 1, 1, 1]
    dist = [0, PLANE, 3 + 2 * core, 2 * PLANE, 7 - 6 * core, 2, 1 + 2 * core, 6, 5 + 2 * core]
    terms = [None] * 18
    acc = None
    ys = None
    qb = q4
    for sel in (late, early):
        acc, out = attend_blocks(
            [modes[j] for j in sel], [dist[j] for j in sel], idx, qb, do4, lse3, delta3, acc,
            [kb[j] for j in sel] + [vb[j] for j in sel])
        for m, j in enumerate(sel):
            terms[j] = out[m]
            terms[9 + j] = out[len(sel) + m]
        if ys is None:
            ys = list(gather_y(terms[:9], n) + gather_y(terms[9:], n))
            (ys[1], ys[3]), qb = lax.optimization_barrier(((ys[1], ys[3]), q4))
    ys = list(ys)
    (ys[0], ys[2]), acc = lax.optimization_barrier(((ys[0], ys[2]), acc))
    grad_k = unroute(terms[:9], ys[0], ys[1], n, half, core)
    grad_v = unroute(terms[9:], ys[2], ys[3], n, half, core)

    dq = (acc * SCALE).astype(jnp.bfloat16).reshape(heads_kv, width, groups, tok)
    grad_query = dq.transpose(3, 0, 2, 1).reshape(tok, heads_q, width)
    return (grad_query, grad_k, grad_v)


def solution(mesh):
    placed = (
        P(("dp", "seq"), None, None),
        P(("dp", "seq"), None, None),
        P(("dp", "seq"), None, None),
        P(("dp", "seq"), None, None),
        P(("dp", "seq"), None, None),
        P(None, ("dp", "seq")),
    )
    return jax.shard_map(
        per_device,
        mesh=mesh,
        in_specs=placed,
        out_specs=(
            P(("dp", "seq"), None, None),
            P(("dp", "seq"), None, None),
            P(("dp", "seq"), None, None),
        ),
        check_vma=False,
    )
```
